32 devices in a mesh: seq: 4 (over y, core), batch: 8 (over z, x).
Axes of the slice: x: 2, y: 2, z: 4, core: 2. Of those that a mesh axis runs over, the one named last changes fastest.
Arguments:
- inputs: bfloat16 [8, 512, 768], P('batch', 'seq'), may hold values from -6 to 6
- cotangent: bfloat16 [8, 512, 768], P('batch', 'seq'), may hold values from -6 to 6
- weight: bfloat16 [768, 2304], replicated, may hold values from -0.125 to 0.125
Outputs:
- grad_input: bfloat16 [8, 512, 768], P('batch', 'seq')
- grad_weight: float32 [768, 2304], P('seq', 'batch')
The draws below stay inside these ranges and needn't reach their ends.
All inputs are finite; a program needn't handle non-finite values.
Results may differ from the reference program's by a relative error of at most 0.0026.
Values may be sent and summed in bfloat16 or wider, within the bound.
No kernel may reach another device: no remote copies, remote signals or barrier semaphores. Data moves between devices by JAX's collectives and lax.ppermute only.
A program may use at most 64 MiB of HBM per device.

```python
import math
import jax
import jax.numpy as jnp
from jax import lax

CI = 768
CO = 768
KW = 3
TAP_SPACING = 64
NSEQS = 8
SEQ_LEN = 512


def strengthened(drawn, stream_key, source, target, blocks, factor):
    def block_of(axis_at):
        return (jnp.arange(drawn.shape[axis_at]) // (drawn.shape[axis_at] // blocks)).reshape((-1,) + (1,) * (drawn.ndim - 1 - axis_at))

    near = jax.random.permutation(stream_key, blocks)[block_of(target)]
    other_side = (block_of(target) + blocks // 2) % blocks
    return jnp.where((block_of(source) == near) | (block_of(source) == other_side), factor * drawn, drawn)


def steps_of(own_key, extent, split, least, top_value):
    def one(position, blocks):
        draws = jax.random.uniform(jax.random.fold_in(jax.random.fold_in(own_key, 6), position), (blocks,), jnp.float32, least / len(split), top_value / len(split))
        return jnp.repeat(jnp.exp(draws), extent[position] // blocks).reshape((-1,) + (1,) * (len(extent) - position - 1))

    level = one(*split[0])
    for cut in split[1:]:
        level = level * one(*cut)
    return level


def scatter_about(rng, shape, width, most, shards=(), kind=jnp.bfloat16):
    level = steps_of(rng, shape, shards, -0.22, 0.18) if shards else 1.0
    values = jax.random.normal(rng, shape, jnp.float32) * width * level
    return jnp.minimum(jnp.maximum(values, -most), most).astype(kind)


def gaussian_with(key, dims, deviation, reach, shards, heavy, kind=jnp.bfloat16):
    array = deviation * jax.random.normal(key, dims, jnp.float32)
    if shards:
        array = array * steps_of(key, dims, shards, -0.22, 0.18)
    return jnp.clip(strengthened(array, jax.random.fold_in(key, 3), *heavy), -reach, reach).astype(kind)


def setup_inputs(seed: int = 0) -> dict:
    keys = jax.random.split(jax.random.key(seed), 4)
    return {
        "inputs": gaussian_with(keys[0], (NSEQS, SEQ_LEN, CI), 1.0, 6.0, ((0, 8), (1, 4)), (0, 2, 8, 2.0)),
        "cotangent": scatter_about(keys[1], (NSEQS, SEQ_LEN, CO), 1.0, 6.0, ((0, 8), (1, 4))),
        "weight": scatter_about(keys[2], (CO, KW * CI), (KW * CI) ** -0.5, 0.125),
    }


def gelu_factors(values):
    normal_cdf = 0.5 * (1.0 + jax.scipy.special.erf(values / math.sqrt(2.0)))
    density = jnp.exp(-0.5 * values * values) / math.sqrt(2.0 * math.pi)
    return (values * normal_cdf, normal_cdf + values * density)

def reference(inputs, cotangent, weight):
    middle_offset = KW // 2
    length = SEQ_LEN

    def one_sequence(total, pair):
        sequence, gradient_list = pair
        values = sequence.astype(jnp.float32)
        activation, deriv = gelu_factors(values)
        act = activation.astype(jnp.bfloat16)
        padded_input = jnp.pad(gradient_list, ((middle_offset * TAP_SPACING, middle_offset * TAP_SPACING), (0, 0)))
        grad_act = jnp.zeros((length, CI), jnp.float32)
        pieces = []
        for tap_index in range(KW):
            window_start = (2 * middle_offset - tap_index) * TAP_SPACING
            window = lax.slice_in_dim(padded_input, window_start, window_start + length, axis=0)
            grad_act = grad_act + jnp.dot(window, weight[:, tap_index * CI:(tap_index + 1) * CI], preferred_element_type=jnp.float32)
            pieces.append(lax.dot_general(window, act, (((0,), (0,)), ((), ())), preferred_element_type=jnp.float32))
        grad_in = (grad_act * deriv).astype(jnp.bfloat16)
        return (total + jnp.concatenate(pieces, axis=1), grad_in)
    start = jnp.zeros((CO, KW * CI), jnp.float32)
    total, grad_input = lax.scan(one_sequence, start, (inputs, cotangent))
    grad_weight = total * (1.0 / math.sqrt(float(NSEQS * SEQ_LEN)))
    return (grad_input, grad_weight)
```

```python
import math

import jax
import jax.numpy as jnp
from jax import lax
from jax.sharding import PartitionSpec as P

KW = 3
TAP_SPACING = 64


def extended_2(x, sides, width):
    for axis, dim in sides:
        peers, length = (lax.axis_size(axis), x.shape[dim])
        up = [(i, (i + 1) % peers) for i in range(peers - 1)]
        down = [(j, i) for i, j in up]
        last = lax.slice_in_dim(x, length - width, length, axis=dim)
        first = lax.slice_in_dim(x, 0, width, axis=dim)
        before = lax.ppermute(last, axis, up)
        after = lax.ppermute(first, axis, down)
        x = jnp.concatenate([before, x, after], axis=dim)
    return x


def gelu_factors(values):
    normal_cdf = 0.5 * (1.0 + jax.scipy.special.erf(values / math.sqrt(2.0)))
    density = jnp.exp(-0.5 * values * values) / math.sqrt(2.0 * math.pi)
    return (values * normal_cdf, normal_cdf + values * density)


def body(inputs, cotangent, weight):
    middle_offset = KW // 2
    reach = middle_offset * TAP_SPACING
    length = inputs.shape[1]
    in_width = inputs.shape[2]
    padded_input = extended_2(cotangent, (("seq", 1),), reach)
    extended = padded_input[0]
    values = inputs[0].astype(jnp.float32)
    activation, deriv = gelu_factors(values)
    act = activation.astype(jnp.bfloat16)
    grad_act = jnp.zeros((length, in_width), jnp.float32)
    for tap_index in range(KW):
        window_start = (2 * middle_offset - tap_index) * TAP_SPACING
        window = lax.slice_in_dim(extended, window_start, window_start + length, axis=0)
        grad_act = grad_act + jnp.dot(
            window,
            weight[:, tap_index * in_width : (tap_index + 1) * in_width],
            preferred_element_type=jnp.float32,
        )
    grad_input = (grad_act * deriv).astype(jnp.bfloat16)[None]
    seq_count = lax.axis_size("seq")
    batch_count = lax.axis_size("batch")
    counted = batch_count * inputs.shape[0] * length * seq_count
    factor = 1.0 / math.sqrt(float(counted))
    owned = lax.all_to_all(cotangent, "seq", split_axis=2, concat_axis=1, tiled=True)[0]
    own_rows = owned.shape[1]
    owned_padded = jnp.pad(owned, ((reach, reach), (0, 0)))
    whole_act = lax.all_gather(act[None], "seq", axis=1, tiled=True)[0]
    count = whole_act.shape[0]
    updated = []
    for tap_index in range(KW):
        offset = 0 + (2 * middle_offset - tap_index) * TAP_SPACING
        window = lax.dynamic_slice_in_dim(owned_padded, offset, count, 0)
        updated.append(
            lax.dot_general(
                window, whole_act, (((0,), (0,)), ((), ())), preferred_element_type=jnp.float32
            )
        )
    taps_sum = jnp.stack(updated, axis=0)
    local_rows = jnp.transpose(taps_sum, (1, 0, 2)).reshape(own_rows, KW * in_width) * factor
    pieces = local_rows.reshape(own_rows, batch_count, -1)
    swapped = lax.all_to_all(pieces, "batch", split_axis=1, concat_axis=1, tiled=True)
    grad_weight = jnp.sum(swapped, axis=1)
    return (grad_input, grad_weight)


def solution(mesh):
    placed = (P("batch", "seq", None), P("batch", "seq", None), P())
    return jax.shard_map(
        body,
        mesh=mesh,
        in_specs=placed,
        out_specs=(P("batch", "seq", None), P("seq", "batch")),
        check_vma=False,
    )
```

```python
import math

import jax
import jax.numpy as jnp
from jax import lax
from jax.sharding import PartitionSpec as P

KW = 3
TAP_SPACING = 64


def extended_2(x, sides, width):
    for axis, dim in sides:
        peers, length = (lax.axis_size(axis), x.shape[dim])
        up = [(i, (i + 1) % peers) for i in range(peers - 1)]
        down = [(j, i) for i, j in up]
        last = lax.slice_in_dim(x, length - width, length, axis=dim)
        first = lax.slice_in_dim(x, 0, width, axis=dim)
        before = lax.ppermute(last, axis, up)
        after = lax.ppermute(first, axis, down)
        x = jnp.concatenate([before, x, after], axis=dim)
    return x


def gelu_factors(values):
    normal_cdf = 0.5 * (1.0 + jax.scipy.special.erf(values / math.sqrt(2.0)))
    density = jnp.exp(-0.5 * values * values) / math.sqrt(2.0 * math.pi)
    return (values * normal_cdf, normal_cdf + values * density)


def reduce_over_batch(rows):
    count = lax.axis_size("batch")
    outer = count // 2
    me = lax.axis_index("batch")
    x = me % 2
    z = me // 2
    blocks = rows.reshape(rows.shape[0], outer, 2, -1)
    mine = lax.dynamic_index_in_dim(blocks, x, axis=2, keepdims=False)
    theirs = lax.dynamic_index_in_dim(blocks, 1 - x, axis=2, keepdims=False)
    pairs = [(i, i ^ 1) for i in range(count)]
    summed = mine + lax.ppermute(theirs, "batch", pairs)
    total = lax.dynamic_index_in_dim(summed, z, axis=1, keepdims=False)
    for shift in range(1, outer):
        target = lax.dynamic_index_in_dim(summed, (z + shift) % outer, axis=1, keepdims=False)
        perm = [(2 * q + p, 2 * ((q + shift) % outer) + p) for q in range(outer) for p in range(2)]
        total = total + lax.ppermute(target, "batch", perm)
    return total


def body(inputs, cotangent, weight):
    middle_offset = KW // 2
    reach = middle_offset * TAP_SPACING
    length = inputs.shape[1]
    in_width = inputs.shape[2]
    padded_input = extended_2(cotangent, (("seq", 1),), reach)
    extended = padded_input[0]
    values = inputs[0].astype(jnp.float32)
    activation, deriv = gelu_factors(values)
    act = activation.astype(jnp.bfloat16)
    grad_act = jnp.zeros((length, in_width), jnp.float32)
    for tap_index in range(KW):
        window_start = (2 * middle_offset - tap_index) * TAP_SPACING
        window = lax.slice_in_dim(extended, window_start, window_start + length, axis=0)
        grad_act = grad_act + jnp.dot(
            window,
            weight[:, tap_index * in_width : (tap_index + 1) * in_width],
            preferred_element_type=jnp.float32,
        )
    grad_input = (grad_act * deriv).astype(jnp.bfloat16)[None]
    seq_count = lax.axis_size("seq")
    batch_count = lax.axis_size("batch")
    counted = batch_count * inputs.shape[0] * length * seq_count
    factor = 1.0 / math.sqrt(float(counted))
    owned = lax.all_to_all(cotangent, "seq", split_axis=2, concat_axis=1, tiled=True)[0]
    own_rows = owned.shape[1]
    owned_padded = jnp.pad(owned, ((reach, reach), (0, 0)))
    whole_act = lax.all_gather(act[None], "seq", axis=1, tiled=True)[0]
    count = whole_act.shape[0]
    updated = []
    for tap_index in range(KW):
        offset = 0 + (2 * middle_offset - tap_index) * TAP_SPACING
        window = lax.dynamic_slice_in_dim(owned_padded, offset, count, 0)
        updated.append(
            lax.dot_general(
                window, whole_act, (((0,), (0,)), ((), ())), preferred_element_type=jnp.float32
            )
        )
    taps_sum = jnp.stack(updated, axis=0)
    local_rows = jnp.transpose(taps_sum, (1, 0, 2)).reshape(own_rows, KW * in_width) * factor
    if batch_count == 8:
        grad_weight = reduce_over_batch(local_rows)
    else:
        pieces = local_rows.reshape(own_rows, batch_count, -1)
        swapped = lax.all_to_all(pieces, "batch", split_axis=1, concat_axis=1, tiled=True)
        grad_weight = jnp.sum(swapped, axis=1)
    return (grad_input, grad_weight)


def solution(mesh):
    placed = (P("batch", "seq", None), P("batch", "seq", None), P())
    return jax.shard_map(
        body,
        mesh=mesh,
        in_specs=placed,
        out_specs=(P("batch", "seq", None), P("seq", "batch")),
        check_vma=False,
    )
```

```python
import math

import jax
import jax.numpy as jnp
from jax import lax
from jax.sharding import PartitionSpec as P

KW = 3
TAP_SPACING = 64
CHUNKS = 4


def extended_2(x, sides, width):
    for axis, dim in sides:
        peers, length = (lax.axis_size(axis), x.shape[dim])
        up = [(i, (i + 1) % peers) for i in range(peers - 1)]
        down = [(j, i) for i, j in up]
        last = lax.slice_in_dim(x, length - width, length, axis=dim)
        first = lax.slice_in_dim(x, 0, width, axis=dim)
        before = lax.ppermute(last, axis, up)
        after = lax.ppermute(first, axis, down)
        x = jnp.concatenate([before, x, after], axis=dim)
    return x


def gelu_factors(values):
    normal_cdf = 0.5 * (1.0 + jax.scipy.special.erf(values / math.sqrt(2.0)))
    density = jnp.exp(-0.5 * values * values) / math.sqrt(2.0 * math.pi)
    return (values * normal_cdf, normal_cdf + values * density)


def reduce_over_batch(rows, chunks):
    count = lax.axis_size("batch")
    outer = count // 2
    me = lax.axis_index("batch")
    x = me % 2
    z = me // 2
    pairs = [(i, i ^ 1) for i in range(count)]
    step = rows.shape[0] // chunks
    results = []
    previous = None
    for chunk in range(chunks):
        part = rows[chunk * step : (chunk + 1) * step]
        blocks = part.reshape(step, outer, 2, -1)
        mine = lax.dynamic_index_in_dim(blocks, x, axis=2, keepdims=False)
        theirs = lax.dynamic_index_in_dim(blocks, 1 - x, axis=2, keepdims=False)
        if previous is not None:
            previous, theirs = lax.optimization_barrier((previous, theirs))
        arrived = lax.ppermute(theirs, "batch", pairs)
        previous = arrived
        summed = mine + arrived
        total = lax.dynamic_index_in_dim(summed, z, axis=1, keepdims=False)
        for shift in range(1, outer):
            target = lax.dynamic_index_in_dim(summed, (z + shift) % outer, axis=1, keepdims=False)
            perm = [(2 * q + p, 2 * ((q + shift) % outer) + p) for q in range(outer) for p in range(2)]
            total = total + lax.ppermute(target, "batch", perm)
        results.append(total)
    return jnp.concatenate(results, axis=0)


def body(inputs, cotangent, weight):
    middle_offset = KW // 2
    reach = middle_offset * TAP_SPACING
    length = inputs.shape[1]
    in_width = inputs.shape[2]
    padded_input = extended_2(cotangent, (("seq", 1),), reach)
    extended = padded_input[0]
    values = inputs[0].astype(jnp.float32)
    activation, deriv = gelu_factors(values)
    act = activation.astype(jnp.bfloat16)
    grad_act = jnp.zeros((length, in_width), jnp.float32)
    for tap_index in range(KW):
        window_start = (2 * middle_offset - tap_index) * TAP_SPACING
        window = lax.slice_in_dim(extended, window_start, window_start + length, axis=0)
        grad_act = grad_act + jnp.dot(
            window,
            weight[:, tap_index * in_width : (tap_index + 1) * in_width],
            preferred_element_type=jnp.float32,
        )
    grad_input = (grad_act * deriv).astype(jnp.bfloat16)[None]
    seq_count = lax.axis_size("seq")
    batch_count = lax.axis_size("batch")
    counted = batch_count * inputs.shape[0] * length * seq_count
    factor = 1.0 / math.sqrt(float(counted))
    owned = lax.all_to_all(cotangent, "seq", split_axis=2, concat_axis=1, tiled=True)[0]
    own_rows = owned.shape[1]
    owned_padded = jnp.pad(owned, ((reach, reach), (0, 0)))
    whole_act = lax.all_gather(act[None], "seq", axis=1, tiled=True)[0]
    count = whole_act.shape[0]
    updated = []
    for tap_index in range(KW):
        offset = 0 + (2 * middle_offset - tap_index) * TAP_SPACING
        window = lax.dynamic_slice_in_dim(owned_padded, offset, count, 0)
        updated.append(
            lax.dot_general(
                window, whole_act, (((0,), (0,)), ((), ())), preferred_element_type=jnp.float32
            )
        )
    taps_sum = jnp.stack(updated, axis=0)
    local_rows = jnp.transpose(taps_sum, (1, 0, 2)).reshape(own_rows, KW * in_width) * factor
    if batch_count == 8:
        grad_weight = reduce_over_batch(local_rows, CHUNKS)
    else:
        pieces = local_rows.reshape(own_rows, batch_count, -1)
        swapped = lax.all_to_all(pieces, "batch", split_axis=1, concat_axis=1, tiled=True)
        grad_weight = jnp.sum(swapped, axis=1)
    return (grad_input, grad_weight)


def solution(mesh):
    placed = (P("batch", "seq", None), P("batch", "seq", None), P())
    return jax.shard_map(
        body,
        mesh=mesh,
        in_specs=placed,
        out_specs=(P("batch", "seq", None), P("seq", "batch")),
        check_vma=False,
    )
```

```python
import math

import jax
import jax.numpy as jnp
from jax import lax
from jax.sharding import PartitionSpec as P

KW = 3
TAP_SPACING = 64
CHUNKS = 2
HEADROOM = 12.0


def extended_2(x, sides, width):
    for axis, dim in sides:
        peers, length = (lax.axis_size(axis), x.shape[dim])
        up = [(i, (i + 1) % peers) for i in range(peers - 1)]
        down = [(j, i) for i, j in up]
        last = lax.slice_in_dim(x, length - width, length, axis=dim)
        first = lax.slice_in_dim(x, 0, width, axis=dim)
        before = lax.ppermute(last, axis, up)
        after = lax.ppermute(first, axis, down)
        x = jnp.concatenate([before, x, after], axis=dim)
    return x


def gelu_factors(values):
    normal_cdf = 0.5 * (1.0 + jax.scipy.special.erf(values / math.sqrt(2.0)))
    density = jnp.exp(-0.5 * values * values) / math.sqrt(2.0 * math.pi)
    return (values * normal_cdf, normal_cdf + values * density)


def encode(values):
    biggest = jnp.maximum(jnp.max(jnp.abs(values)), 1e-30)
    exponent = jnp.floor(jnp.log2(biggest))
    scaled = (values * jnp.exp2(HEADROOM - exponent)).astype(jnp.float16)
    tag = jnp.full((1,) + values.shape[1:], exponent, jnp.float16)
    return jnp.concatenate([tag, scaled], axis=0)


def decode(packed):
    exponent = packed[0].reshape(-1)[0].astype(jnp.float32)
    return packed[1:].astype(jnp.float32) * jnp.exp2(exponent - HEADROOM)


def send(values, perm):
    return decode(lax.ppermute(encode(values), "batch", perm))


def reduce_over_batch(rows, chunks):
    count = lax.axis_size("batch")
    outer = count // 2
    me = lax.axis_index("batch")
    x = me % 2
    z = me // 2
    pairs = [(i, i ^ 1) for i in range(count)]
    step = rows.shape[0] // chunks

    def finish(mine, packed):
        summed = mine + decode(packed)
        total = lax.dynamic_index_in_dim(summed, z, axis=1, keepdims=False)
        for shift in range(1, outer):
            target = lax.dynamic_index_in_dim(summed, (z + shift) % outer, axis=1, keepdims=False)
            perm = [(2 * q + p, 2 * ((q + shift) % outer) + p) for q in range(outer) for p in range(2)]
            total = total + send(target, perm)
        return total

    results = []
    pending = None
    for chunk in range(chunks):
        part = rows[chunk * step : (chunk + 1) * step]
        blocks = part.reshape(step, outer, 2, -1)
        mine = lax.dynamic_index_in_dim(blocks, x, axis=2, keepdims=False)
        theirs = encode(lax.dynamic_index_in_dim(blocks, 1 - x, axis=2, keepdims=False))
        if pending is not None:
            kept, arrived = pending
            arrived, theirs = lax.optimization_barrier((arrived, theirs))
            results.append(finish(kept, arrived))
        pending = (mine, lax.ppermute(theirs, "batch", pairs))
    results.append(finish(*pending))
    return jnp.concatenate(results, axis=0)


def body(inputs, cotangent, weight):
    middle_offset = KW // 2
    reach = middle_offset * TAP_SPACING
    length = inputs.shape[1]
    in_width = inputs.shape[2]
    padded_input = extended_2(cotangent, (("seq", 1),), reach)
    extended = padded_input[0]
    values = inputs[0].astype(jnp.float32)
    activation, deriv = gelu_factors(values)
    act = activation.astype(jnp.bfloat16)
    grad_act = jnp.zeros((length, in_width), jnp.float32)
    for tap_index in range(KW):
        window_start = (2 * middle_offset - tap_index) * TAP_SPACING
        window = lax.slice_in_dim(extended, window_start, window_start + length, axis=0)
        grad_act = grad_act + jnp.dot(
            window,
            weight[:, tap_index * in_width : (tap_index + 1) * in_width],
            preferred_element_type=jnp.float32,
        )
    grad_input = (grad_act * deriv).astype(jnp.bfloat16)[None]
    seq_count = lax.axis_size("seq")
    batch_count = lax.axis_size("batch")
    counted = batch_count * inputs.shape[0] * length * seq_count
    factor = 1.0 / math.sqrt(float(counted))
    owned = lax.all_to_all(cotangent, "seq", split_axis=2, concat_axis=1, tiled=True)[0]
    own_rows = owned.shape[1]
    owned_padded = jnp.pad(owned, ((reach, reach), (0, 0)))
    whole_act = lax.all_gather(act[None], "seq", axis=1, tiled=True)[0]
    count = whole_act.shape[0]
    updated = []
    for tap_index in range(KW):
        offset = 0 + (2 * middle_offset - tap_index) * TAP_SPACING
        window = lax.dynamic_slice_in_dim(owned_padded, offset, count, 0)
        updated.append(
            lax.dot_general(
                window, whole_act, (((0,), (0,)), ((), ())), preferred_element_type=jnp.float32
            )
        )
    taps_sum = jnp.stack(updated, axis=0)
    local_rows = jnp.transpose(taps_sum, (1, 0, 2)).reshape(own_rows, KW * in_width) * factor
    if batch_count == 8:
        grad_weight = reduce_over_batch(local_rows, CHUNKS)
    else:
        pieces = local_rows.reshape(own_rows, batch_count, -1)
        swapped = lax.all_to_all(pieces, "batch", split_axis=1, concat_axis=1, tiled=True)
        grad_weight = jnp.sum(swapped, axis=1)
    return (grad_input, grad_weight)


def solution(mesh):
    placed = (P("batch", "seq", None), P("batch", "seq", None), P())
    return jax.shard_map(
        body,
        mesh=mesh,
        in_specs=placed,
        out_specs=(P("batch", "seq", None), P("seq", "batch")),
        check_vma=False,
    )
```

```python
import math

import jax
import jax.numpy as jnp
from jax import lax
from jax.sharding import PartitionSpec as P

KW = 3
TAP_SPACING = 64
CHUNKS = 1
HEADROOM = 12.0


def extended_2(x, sides, width):
    for axis, dim in sides:
        peers, length = (lax.axis_size(axis), x.shape[dim])
        up = [(i, (i + 1) % peers) for i in range(peers - 1)]
        down = [(j, i) for i, j in up]
        last = lax.slice_in_dim(x, length - width, length, axis=dim)
        first = lax.slice_in_dim(x, 0, width, axis=dim)
        before = lax.ppermute(last, axis, up)
        after = lax.ppermute(first, axis, down)
        x = jnp.concatenate([before, x, after], axis=dim)
    return x


def gelu_factors(values):
    normal_cdf = 0.5 * (1.0 + jax.scipy.special.erf(values / math.sqrt(2.0)))
    density = jnp.exp(-0.5 * values * values) / math.sqrt(2.0 * math.pi)
    return (values * normal_cdf, normal_cdf + values * density)


def encode(values):
    biggest = jnp.maximum(jnp.max(jnp.abs(values)), 1e-30)
    exponent = jnp.floor(jnp.log2(biggest))
    scaled = (values * jnp.exp2(HEADROOM - exponent)).astype(jnp.float16)
    tag = jnp.full((1,) + values.shape[1:], exponent, jnp.float16)
    return jnp.concatenate([tag, scaled], axis=0)


def decode(packed):
    exponent = packed[0].reshape(-1)[0].astype(jnp.float32)
    return packed[1:].astype(jnp.float32) * jnp.exp2(exponent - HEADROOM)


def send(values, perm):
    return decode(lax.ppermute(encode(values), "batch", perm))


def reduce_over_batch(rows, chunks):
    count = lax.axis_size("batch")
    outer = count // 2
    me = lax.axis_index("batch")
    x = me % 2
    z = me // 2
    pairs = [(i, i ^ 1) for i in range(count)]
    step = rows.shape[0] // chunks

    def finish(mine, packed):
        summed = mine + decode(packed)
        total = lax.dynamic_index_in_dim(summed, z, axis=1, keepdims=False)
        for shift in range(1, outer):
            target = lax.dynamic_index_in_dim(summed, (z + shift) % outer, axis=1, keepdims=False)
            perm = [(2 * q + p, 2 * ((q + shift) % outer) + p) for q in range(outer) for p in range(2)]
            total = total + send(target, perm)
        return total

    results = []
    pending = None
    for chunk in range(chunks):
        part = rows[chunk * step : (chunk + 1) * step]
        blocks = part.reshape(step, outer, 2, -1)
        mine = lax.dynamic_index_in_dim(blocks, x, axis=2, keepdims=False)
        theirs = encode(lax.dynamic_index_in_dim(blocks, 1 - x, axis=2, keepdims=False))
        if pending is not None:
            kept, arrived = pending
            arrived, theirs = lax.optimization_barrier((arrived, theirs))
            results.append(finish(kept, arrived))
        pending = (mine, lax.ppermute(theirs, "batch", pairs))
    results.append(finish(*pending))
    return jnp.concatenate(results, axis=0)


def body(inputs, cotangent, weight):
    middle_offset = KW // 2
    reach = middle_offset * TAP_SPACING
    length = inputs.shape[1]
    in_width = inputs.shape[2]
    values = inputs[0].astype(jnp.float32)
    activation, deriv = gelu_factors(values)
    act = activation.astype(jnp.bfloat16)
    seq_count = lax.axis_size("seq")
    batch_count = lax.axis_size("batch")
    counted = batch_count * inputs.shape[0] * length * seq_count
    factor = 1.0 / math.sqrt(float(counted))
    owned = lax.all_to_all(cotangent, "seq", split_axis=2, concat_axis=1, tiled=True)[0]
    own_rows = owned.shape[1]
    owned_padded = jnp.pad(owned, ((reach, reach), (0, 0)))
    whole_act = lax.all_gather(act[None], "seq", axis=1, tiled=True)[0]
    count = whole_act.shape[0]
    updated = []
    for tap_index in range(KW):
        offset = 0 + (2 * middle_offset - tap_index) * TAP_SPACING
        window = lax.dynamic_slice_in_dim(owned_padded, offset, count, 0)
        updated.append(
            lax.dot_general(
                window, whole_act, (((0,), (0,)), ((), ())), preferred_element_type=jnp.float32
            )
        )
    taps_sum = jnp.stack(updated, axis=0)
    local_rows = jnp.transpose(taps_sum, (1, 0, 2)).reshape(own_rows, KW * in_width) * factor
    local_rows, cotangent, deriv = lax.optimization_barrier((local_rows, cotangent, deriv))
    padded_input = extended_2(cotangent, (("seq", 1),), reach)
    extended = padded_input[0]
    grad_act = jnp.zeros((length, in_width), jnp.float32)
    for tap_index in range(KW):
        window_start = (2 * middle_offset - tap_index) * TAP_SPACING
        window = lax.slice_in_dim(extended, window_start, window_start + length, axis=0)
        grad_act = grad_act + jnp.dot(
            window,
            weight[:, tap_index * in_width : (tap_index + 1) * in_width],
            preferred_element_type=jnp.float32,
        )
    grad_input = (grad_act * deriv).astype(jnp.bfloat16)[None]
    if batch_count == 8:
        grad_weight = reduce_over_batch(local_rows, CHUNKS)
    else:
        pieces = local_rows.reshape(own_rows, batch_count, -1)
        swapped = lax.all_to_all(pieces, "batch", split_axis=1, concat_axis=1, tiled=True)
        grad_weight = jnp.sum(swapped, axis=1)
    return (grad_input, grad_weight)


def solution(mesh):
    placed = (P("batch", "seq", None), P("batch", "seq", None), P())
    return jax.shard_map(
        body,
        mesh=mesh,
        in_specs=placed,
        out_specs=(P("batch", "seq", None), P("seq", "batch")),
        check_vma=False,
    )
```

```python
import math

import jax
import jax.numpy as jnp
from jax import lax
from jax.sharding import PartitionSpec as P

KW = 3
TAP_SPACING = 64
HEADROOM = 12.0
TAG = 16


def extended_2(x, sides, width):
    for axis, dim in sides:
        peers, length = (lax.axis_size(axis), x.shape[dim])
        up = [(i, (i + 1) % peers) for i in range(peers - 1)]
        down = [(j, i) for i, j in up]
        last = lax.slice_in_dim(x, length - width, length, axis=dim)
        first = lax.slice_in_dim(x, 0, width, axis=dim)
        before = lax.ppermute(last, axis, up)
        after = lax.ppermute(first, axis, down)
        x = jnp.concatenate([before, x, after], axis=dim)
    return x


def gelu_factors(values):
    normal_cdf = 0.5 * (1.0 + jax.scipy.special.erf(values / math.sqrt(2.0)))
    density = jnp.exp(-0.5 * values * values) / math.sqrt(2.0 * math.pi)
    return (values * normal_cdf, normal_cdf + values * density)


def encode(values):
    biggest = jnp.maximum(jnp.max(jnp.abs(values)), 1e-30)
    exponent = jnp.floor(jnp.log2(biggest))
    scaled = (values * jnp.exp2(HEADROOM - exponent)).astype(jnp.float16)
    tag = jnp.full(values.shape[:-2] + (TAG, values.shape[-1]), exponent, jnp.float16)
    return jnp.concatenate([scaled, tag], axis=-2)


def decode(packed):
    exponent = packed[(0,) * (packed.ndim - 2) + (-TAG, 0)].astype(jnp.float32)
    return packed[..., :-TAG, :].astype(jnp.float32) * jnp.exp2(exponent - HEADROOM)


def send(values, perm):
    return decode(lax.ppermute(encode(values), "batch", perm))


def reduce_over_batch(columns):
    count = lax.axis_size("batch")
    outer = count // 2
    me = lax.axis_index("batch")
    x = me % 2
    z = me // 2
    pairs = [(i, i ^ 1) for i in range(count)]
    blocks = columns.reshape(outer, 2, -1, columns.shape[1])
    mine = lax.dynamic_index_in_dim(blocks, x, axis=1, keepdims=False)
    theirs = lax.dynamic_index_in_dim(blocks, 1 - x, axis=1, keepdims=False)
    summed = mine + send(theirs, pairs)
    total = lax.dynamic_index_in_dim(summed, z, axis=0, keepdims=False)
    for shift in range(1, outer):
        target = lax.dynamic_index_in_dim(summed, (z + shift) % outer, axis=0, keepdims=False)
        perm = [(2 * q + p, 2 * ((q + shift) % outer) + p) for q in range(outer) for p in range(2)]
        total = total + send(target, perm)
    return total.T


def body(inputs, cotangent, weight):
    middle_offset = KW // 2
    reach = middle_offset * TAP_SPACING
    length = inputs.shape[1]
    in_width = inputs.shape[2]
    values = inputs[0].astype(jnp.float32)
    activation, deriv = gelu_factors(values)
    act = activation.astype(jnp.bfloat16)
    seq_count = lax.axis_size("seq")
    batch_count = lax.axis_size("batch")
    counted = batch_count * inputs.shape[0] * length * seq_count
    factor = 1.0 / math.sqrt(float(counted))
    owned = lax.all_to_all(cotangent, "seq", split_axis=2, concat_axis=1, tiled=True)[0]
    own_rows = owned.shape[1]
    owned_padded = jnp.pad(owned, ((reach, reach), (0, 0)))
    whole_act = lax.all_gather(act[None], "seq", axis=1, tiled=True)[0]
    count = whole_act.shape[0]
    updated = []
    for tap_index in range(KW):
        offset = 0 + (2 * middle_offset - tap_index) * TAP_SPACING
        window = lax.dynamic_slice_in_dim(owned_padded, offset, count, 0)
        updated.append(
            lax.dot_general(
                whole_act, window, (((0,), (0,)), ((), ())), preferred_element_type=jnp.float32
            )
        )
    local_columns = jnp.concatenate(updated, axis=0) * factor
    local_columns, cotangent, deriv = lax.optimization_barrier((local_columns, cotangent, deriv))
    padded_input = extended_2(cotangent, (("seq", 1),), reach)
    extended = padded_input[0]
    grad_act = jnp.zeros((length, in_width), jnp.float32)
    for tap_index in range(KW):
        window_start = (2 * middle_offset - tap_index) * TAP_SPACING
        window = lax.slice_in_dim(extended, window_start, window_start + length, axis=0)
        grad_act = grad_act + jnp.dot(
            window,
            weight[:, tap_index * in_width : (tap_index + 1) * in_width],
            preferred_element_type=jnp.float32,
        )
    grad_input = (grad_act * deriv).astype(jnp.bfloat16)[None]
    if batch_count == 8:
        grad_weight = reduce_over_batch(local_columns)
    else:
        pieces = local_columns.reshape(batch_count, -1, own_rows)
        swapped = lax.all_to_all(pieces, "batch", split_axis=0, concat_axis=0, tiled=True)
        grad_weight = jnp.sum(swapped, axis=0).T
    return (grad_input, grad_weight)


def solution(mesh):
    placed = (P("batch", "seq", None), P("batch", "seq", None), P())
    return jax.shard_map(
        body,
        mesh=mesh,
        in_specs=placed,
        out_specs=(P("batch", "seq", None), P("seq", "batch")),
        check_vma=False,
    )
```

```python
import math

import jax
import jax.numpy as jnp
from jax import lax
from jax.experimental.layout import Layout, with_layout_constraint
from jax.sharding import PartitionSpec as P

KW = 3
TAP_SPACING = 64
HEADROOM = 12.0
TAG = 16


def extended_2(x, sides, width):
    for axis, dim in sides:
        peers, length = (lax.axis_size(axis), x.shape[dim])
        up = [(i, (i + 1) % peers) for i in range(peers - 1)]
        down = [(j, i) for i, j in up]
        last = lax.slice_in_dim(x, length - width, length, axis=dim)
        first = lax.slice_in_dim(x, 0, width, axis=dim)
        before = lax.ppermute(last, axis, up)
        after = lax.ppermute(first, axis, down)
        x = jnp.concatenate([before, x, after], axis=dim)
    return x


def gelu_factors(values):
    normal_cdf = 0.5 * (1.0 + jax.scipy.special.erf(values / math.sqrt(2.0)))
    density = jnp.exp(-0.5 * values * values) / math.sqrt(2.0 * math.pi)
    return (values * normal_cdf, normal_cdf + values * density)


def encode(values):
    flat = values.reshape(-1, values.shape[-1])
    biggest = jnp.maximum(jnp.max(jnp.abs(flat)), 1e-30)
    exponent = jnp.floor(jnp.log2(biggest))
    scaled = (flat * jnp.exp2(HEADROOM - exponent)).astype(jnp.float16)
    tag = jnp.full((TAG, flat.shape[-1]), exponent, jnp.float16)
    return with_layout_constraint(jnp.concatenate([scaled, tag], axis=0), Layout((0, 1)))


def decode(packed, shape):
    exponent = packed[-TAG, 0].astype(jnp.float32)
    values = packed[:-TAG].astype(jnp.float32) * jnp.exp2(exponent - HEADROOM)
    return values.reshape(shape)


def send(values, perm):
    arrived = lax.ppermute(encode(values), "batch", perm)
    return decode(with_layout_constraint(arrived, Layout((0, 1))), values.shape)


def reduce_over_batch(columns):
    count = lax.axis_size("batch")
    outer = count // 2
    me = lax.axis_index("batch")
    x = me % 2
    z = me // 2
    pairs = [(i, i ^ 1) for i in range(count)]
    blocks = columns.reshape(outer, 2, -1, columns.shape[1])
    mine = lax.dynamic_index_in_dim(blocks, x, axis=1, keepdims=False)
    theirs = lax.dynamic_index_in_dim(blocks, 1 - x, axis=1, keepdims=False)
    summed = with_layout_constraint(mine + send(theirs, pairs), Layout((0, 1, 2)))
    total = lax.dynamic_index_in_dim(summed, z, axis=0, keepdims=False)
    for shift in range(1, outer):
        target = lax.dynamic_index_in_dim(summed, (z + shift) % outer, axis=0, keepdims=False)
        perm = [(2 * q + p, 2 * ((q + shift) % outer) + p) for q in range(outer) for p in range(2)]
        total = total + send(target, perm)
    return with_layout_constraint(total, Layout((0, 1))).T


def body(inputs, cotangent, weight):
    middle_offset = KW // 2
    reach = middle_offset * TAP_SPACING
    length = inputs.shape[1]
    in_width = inputs.shape[2]
    values = inputs[0].astype(jnp.float32)
    activation, deriv = gelu_factors(values)
    act = activation.astype(jnp.bfloat16)
    seq_count = lax.axis_size("seq")
    batch_count = lax.axis_size("batch")
    counted = batch_count * inputs.shape[0] * length * seq_count
    factor = 1.0 / math.sqrt(float(counted))
    owned = lax.all_to_all(cotangent, "seq", split_axis=2, concat_axis=1, tiled=True)[0]
    own_rows = owned.shape[1]
    owned_padded = jnp.pad(owned, ((reach, reach), (0, 0)))
    whole_act = lax.all_gather(act[None], "seq", axis=1, tiled=True)[0]
    count = whole_act.shape[0]
    updated = []
    for tap_index in range(KW):
        offset = 0 + (2 * middle_offset - tap_index) * TAP_SPACING
        window = lax.dynamic_slice_in_dim(owned_padded, offset, count, 0)
        updated.append(
            lax.dot_general(
                whole_act, window, (((0,), (0,)), ((), ())), preferred_element_type=jnp.float32
            )
        )
    local_columns = jnp.concatenate(updated, axis=0) * factor
    local_columns = with_layout_constraint(local_columns, Layout((0, 1)))
    local_columns, cotangent, deriv = lax.optimization_barrier((local_columns, cotangent, deriv))
    padded_input = extended_2(cotangent, (("seq", 1),), reach)
    extended = padded_input[0]
    grad_act = jnp.zeros((length, in_width), jnp.float32)
    for tap_index in range(KW):
        window_start = (2 * middle_offset - tap_index) * TAP_SPACING
        window = lax.slice_in_dim(extended, window_start, window_start + length, axis=0)
        grad_act = grad_act + jnp.dot(
            window,
            weight[:, tap_index * in_width : (tap_index + 1) * in_width],
            preferred_element_type=jnp.float32,
        )
    grad_input = (grad_act * deriv).astype(jnp.bfloat16)[None]
    if batch_count == 8:
        grad_weight = reduce_over_batch(local_columns)
    else:
        pieces = local_columns.reshape(batch_count, -1, own_rows)
        swapped = lax.all_to_all(pieces, "batch", split_axis=0, concat_axis=0, tiled=True)
        grad_weight = jnp.sum(swapped, axis=0).T
    return (grad_input, grad_weight)


def solution(mesh):
    placed = (P("batch", "seq", None), P("batch", "seq", None), P())
    return jax.shard_map(
        body,
        mesh=mesh,
        in_specs=placed,
        out_specs=(P("batch", "seq", None), P("seq", "batch")),
        check_vma=False,
    )
```

```python
import math

import jax
import jax.numpy as jnp
from jax import lax
from jax.experimental.layout import Layout, with_layout_constraint
from jax.sharding import PartitionSpec as P

KW = 3
TAP_SPACING = 64
HEADROOM = 12.0
TAG = 16


def extended_2(x, sides, width):
    for axis, dim in sides:
        peers, length = (lax.axis_size(axis), x.shape[dim])
        up = [(i, (i + 1) % peers) for i in range(peers - 1)]
        down = [(j, i) for i, j in up]
        last = lax.slice_in_dim(x, length - width, length, axis=dim)
        first = lax.slice_in_dim(x, 0, width, axis=dim)
        before = lax.ppermute(last, axis, up)
        after = lax.ppermute(first, axis, down)
        x = jnp.concatenate([before, x, after], axis=dim)
    return x


def gelu_factors(values):
    normal_cdf = 0.5 * (1.0 + jax.scipy.special.erf(values / math.sqrt(2.0)))
    density = jnp.exp(-0.5 * values * values) / math.sqrt(2.0 * math.pi)
    return (values * normal_cdf, normal_cdf + values * density)


def encode(values):
    flat = values.reshape(-1, values.shape[-1])
    biggest = jnp.maximum(jnp.max(jnp.abs(flat)), 1e-30)
    exponent = jnp.floor(jnp.log2(biggest))
    scaled = (flat * jnp.exp2(HEADROOM - exponent)).astype(jnp.float16)
    tag = jnp.full((TAG, flat.shape[-1]), exponent, jnp.float16)
    return with_layout_constraint(jnp.concatenate([scaled, tag], axis=0), Layout((0, 1)))


def decode(packed, shape):
    exponent = packed[-TAG, 0].astype(jnp.float32)
    values = packed[:-TAG].astype(jnp.float32) * jnp.exp2(exponent - HEADROOM)
    return values.reshape(shape)


def send(values, perm):
    arrived = lax.ppermute(encode(values), "batch", perm)
    return decode(with_layout_constraint(arrived, Layout((0, 1))), values.shape)


def reduce_over_batch(columns):
    count = lax.axis_size("batch")
    outer = count // 2
    me = lax.axis_index("batch")
    x = me % 2
    z = me // 2
    pairs = [(i, i ^ 1) for i in range(count)]
    blocks = columns.reshape(outer, 2, -1, columns.shape[1])
    mine = lax.dynamic_index_in_dim(blocks, x, axis=1, keepdims=False)
    theirs = lax.dynamic_index_in_dim(blocks, 1 - x, axis=1, keepdims=False)
    summed = with_layout_constraint(mine + send(theirs, pairs), Layout((0, 1, 2)))
    total = lax.dynamic_index_in_dim(summed, z, axis=0, keepdims=False)
    for shift in range(1, outer):
        target = lax.dynamic_index_in_dim(summed, (z + shift) % outer, axis=0, keepdims=False)
        perm = [(2 * q + p, 2 * ((q + shift) % outer) + p) for q in range(outer) for p in range(2)]
        total = total + send(target, perm)
    return with_layout_constraint(total, Layout((0, 1))).T


def body(inputs, cotangent, weight):
    middle_offset = KW // 2
    reach = middle_offset * TAP_SPACING
    length = inputs.shape[1]
    in_width = inputs.shape[2]
    values = inputs[0].astype(jnp.float32)
    activation, deriv = gelu_factors(values)
    act = activation.astype(jnp.bfloat16)
    seq_count = lax.axis_size("seq")
    batch_count = lax.axis_size("batch")
    counted = batch_count * inputs.shape[0] * length * seq_count
    factor = 1.0 / math.sqrt(float(counted))
    both = lax.all_gather(jnp.concatenate([act[None], cotangent], axis=0), "seq", axis=1, tiled=True)
    whole_act = both[0]
    own_rows = cotangent.shape[2] // seq_count
    owned = lax.dynamic_slice_in_dim(both[1], lax.axis_index("seq") * own_rows, own_rows, axis=1)
    owned_padded = jnp.pad(owned, ((reach, reach), (0, 0)))
    count = whole_act.shape[0]
    updated = []
    for tap_index in range(KW):
        offset = 0 + (2 * middle_offset - tap_index) * TAP_SPACING
        window = lax.dynamic_slice_in_dim(owned_padded, offset, count, 0)
        updated.append(
            lax.dot_general(
                whole_act, window, (((0,), (0,)), ((), ())), preferred_element_type=jnp.float32
            )
        )
    local_columns = jnp.concatenate(updated, axis=0) * factor
    local_columns = with_layout_constraint(local_columns, Layout((0, 1)))
    padded_input = extended_2(cotangent, (("seq", 1),), reach)
    extended = padded_input[0]
    grad_act = jnp.zeros((length, in_width), jnp.float32)
    for tap_index in range(KW):
        window_start = (2 * middle_offset - tap_index) * TAP_SPACING
        window = lax.slice_in_dim(extended, window_start, window_start + length, axis=0)
        grad_act = grad_act + jnp.dot(
            window,
            weight[:, tap_index * in_width : (tap_index + 1) * in_width],
            preferred_element_type=jnp.float32,
        )
    grad_input = (grad_act * deriv).astype(jnp.bfloat16)[None]
    if batch_count == 8:
        grad_weight = reduce_over_batch(local_columns)
    else:
        pieces = local_columns.reshape(batch_count, -1, own_rows)
        swapped = lax.all_to_all(pieces, "batch", split_axis=0, concat_axis=0, tiled=True)
        grad_weight = jnp.sum(swapped, axis=0).T
    return (grad_input, grad_weight)


def solution(mesh):
    placed = (P("batch", "seq", None), P("batch", "seq", None), P())
    return jax.shard_map(
        body,
        mesh=mesh,
        in_specs=placed,
        out_specs=(P("batch", "seq", None), P("seq", "batch")),
        check_vma=False,
    )
```

```python
import math

import jax
import jax.numpy as jnp
from jax import lax
from jax.experimental.layout import Layout, with_layout_constraint
from jax.sharding import PartitionSpec as P

KW = 3
TAP_SPACING = 64
HEADROOM = 12.0
TAG = 16


def extended_2(x, sides, width):
    for axis, dim in sides:
        peers, length = (lax.axis_size(axis), x.shape[dim])
        up = [(i, (i + 1) % peers) for i in range(peers - 1)]
        down = [(j, i) for i, j in up]
        last = lax.slice_in_dim(x, length - width, length, axis=dim)
        first = lax.slice_in_dim(x, 0, width, axis=dim)
        before = lax.ppermute(last, axis, up)
        after = lax.ppermute(first, axis, down)
        x = jnp.concatenate([before, x, after], axis=dim)
    return x


def gelu_factors(values):
    normal_cdf = 0.5 * (1.0 + jax.scipy.special.erf(values / math.sqrt(2.0)))
    density = jnp.exp(-0.5 * values * values) / math.sqrt(2.0 * math.pi)
    return (values * normal_cdf, normal_cdf + values * density)


def encode(values):
    flat = values.reshape(-1, values.shape[-1])
    biggest = jnp.maximum(jnp.max(jnp.abs(flat)), 1e-30)
    exponent = jnp.floor(jnp.log2(biggest))
    scaled = (flat * jnp.exp2(HEADROOM - exponent)).astype(jnp.float16)
    tag = jnp.full((TAG, flat.shape[-1]), exponent, jnp.float16)
    return with_layout_constraint(jnp.concatenate([scaled, tag], axis=0), Layout((0, 1)))


def decode(packed, shape):
    exponent = packed[-TAG, 0].astype(jnp.float32)
    values = packed[:-TAG].astype(jnp.float32) * jnp.exp2(exponent - HEADROOM)
    return values.reshape(shape)


def send(values, perm):
    arrived = lax.ppermute(encode(values), "batch", perm)
    return decode(with_layout_constraint(arrived, Layout((0, 1))), values.shape)


def reduce_over_batch(columns):
    count = lax.axis_size("batch")
    outer = count // 2
    me = lax.axis_index("batch")
    x = me % 2
    z = me // 2
    pairs = [(i, i ^ 1) for i in range(count)]
    perms = [
        [(2 * q + p, 2 * ((q + shift) % outer) + p) for q in range(outer) for p in range(2)]
        for shift in range(1, outer)
    ]
    blocks = columns.reshape(outer, 2, -1, columns.shape[1])
    half = blocks.shape[2] // 2
    mine = lax.dynamic_index_in_dim(blocks, x, axis=1, keepdims=False)
    theirs = lax.dynamic_index_in_dim(blocks, 1 - x, axis=1, keepdims=False)
    parts = [(mine[:, :half], theirs[:, :half]), (mine[:, half:], theirs[:, half:])]

    def z_packets(summed):
        targets = [
            lax.dynamic_index_in_dim(summed, (z + shift) % outer, axis=0, keepdims=False)
            for shift in range(1, outer)
        ]
        return [encode(t) for t in targets]

    def z_finish(summed, packets):
        total = lax.dynamic_index_in_dim(summed, z, axis=0, keepdims=False)
        for packet, perm in zip(packets, perms):
            arrived = lax.ppermute(packet, "batch", perm)
            total = total + decode(with_layout_constraint(arrived, Layout((0, 1))), total.shape)
        return total

    first_mine, first_theirs = parts[0]
    second_mine, second_theirs = parts[1]
    first_summed = first_mine + send(first_theirs, pairs)
    first_packets = z_packets(first_summed)
    second_packet = encode(second_theirs)
    first_packets, second_packet = lax.optimization_barrier((first_packets, second_packet))
    arrived = lax.ppermute(second_packet, "batch", pairs)
    first_total = z_finish(first_summed, first_packets)
    second_summed = second_mine + decode(with_layout_constraint(arrived, Layout((0, 1))), second_theirs.shape)
    second_total = z_finish(second_summed, z_packets(second_summed))
    total = jnp.concatenate([first_total, second_total], axis=0)
    return with_layout_constraint(total, Layout((0, 1))).T


def body(inputs, cotangent, weight):
    middle_offset = KW // 2
    reach = middle_offset * TAP_SPACING
    length = inputs.shape[1]
    in_width = inputs.shape[2]
    values = inputs[0].astype(jnp.float32)
    activation, deriv = gelu_factors(values)
    act = activation.astype(jnp.bfloat16)
    seq_count = lax.axis_size("seq")
    batch_count = lax.axis_size("batch")
    counted = batch_count * inputs.shape[0] * length * seq_count
    factor = 1.0 / math.sqrt(float(counted))
    owned = lax.all_to_all(cotangent, "seq", split_axis=2, concat_axis=1, tiled=True)[0]
    own_rows = owned.shape[1]
    owned_padded = jnp.pad(owned, ((reach, reach), (0, 0)))
    whole_act = lax.all_gather(act[None], "seq", axis=1, tiled=True)[0]
    count = whole_act.shape[0]
    updated = []
    for tap_index in range(KW):
        offset = 0 + (2 * middle_offset - tap_index) * TAP_SPACING
        window = lax.dynamic_slice_in_dim(owned_padded, offset, count, 0)
        updated.append(
            lax.dot_general(
                whole_act, window, (((0,), (0,)), ((), ())), preferred_element_type=jnp.float32
            )
        )
    local_columns = jnp.concatenate(updated, axis=0) * factor
    local_columns = with_layout_constraint(local_columns, Layout((0, 1)))
    local_columns, cotangent, deriv = lax.optimization_barrier((local_columns, cotangent, deriv))
    padded_input = extended_2(cotangent, (("seq", 1),), reach)
    extended = padded_input[0]
    grad_act = jnp.zeros((length, in_width), jnp.float32)
    for tap_index in range(KW):
        window_start = (2 * middle_offset - tap_index) * TAP_SPACING
        window = lax.slice_in_dim(extended, window_start, window_start + length, axis=0)
        grad_act = grad_act + jnp.dot(
            window,
            weight[:, tap_index * in_width : (tap_index + 1) * in_width],
            preferred_element_type=jnp.float32,
        )
    grad_input = (grad_act * deriv).astype(jnp.bfloat16)[None]
    if batch_count == 8:
        grad_weight = reduce_over_batch(local_columns)
    else:
        pieces = local_columns.reshape(batch_count, -1, own_rows)
        swapped = lax.all_to_all(pieces, "batch", split_axis=0, concat_axis=0, tiled=True)
        grad_weight = jnp.sum(swapped, axis=0).T
    return (grad_input, grad_weight)


def solution(mesh):
    placed = (P("batch", "seq", None), P("batch", "seq", None), P())
    return jax.shard_map(
        body,
        mesh=mesh,
        in_specs=placed,
        out_specs=(P("batch", "seq", None), P("seq", "batch")),
        check_vma=False,
    )
```

```python
import math

import jax
import jax.numpy as jnp
from jax import lax
from jax.experimental.layout import Layout, with_layout_constraint
from jax.sharding import PartitionSpec as P

KW = 3
TAP_SPACING = 64
HEADROOM = 12.0
TAG = 16


def extended_2(x, sides, width):
    for axis, dim in sides:
        peers, length = (lax.axis_size(axis), x.shape[dim])
        up = [(i, (i + 1) % peers) for i in range(peers - 1)]
        down = [(j, i) for i, j in up]
        last = lax.slice_in_dim(x, length - width, length, axis=dim)
        first = lax.slice_in_dim(x, 0, width, axis=dim)
        before = lax.ppermute(last, axis, up)
        after = lax.ppermute(first, axis, down)
        x = jnp.concatenate([before, x, after], axis=dim)
    return x


def gelu_factors(values):
    normal_cdf = 0.5 * (1.0 + jax.scipy.special.erf(values / math.sqrt(2.0)))
    density = jnp.exp(-0.5 * values * values) / math.sqrt(2.0 * math.pi)
    return (values * normal_cdf, normal_cdf + values * density)


def encode(values):
    flat = values.reshape(-1, values.shape[-1])
    biggest = jnp.maximum(jnp.max(jnp.abs(flat)), 1e-30)
    exponent = jnp.floor(jnp.log2(biggest))
    scaled = (flat * jnp.exp2(HEADROOM - exponent)).astype(jnp.float16)
    tag = jnp.full((TAG, flat.shape[-1]), exponent, jnp.float16)
    return with_layout_constraint(jnp.concatenate([scaled, tag], axis=0), Layout((0, 1)))


def decode(packed, shape):
    exponent = packed[-TAG, 0].astype(jnp.float32)
    values = packed[:-TAG].astype(jnp.float32) * jnp.exp2(exponent - HEADROOM)
    return values.reshape(shape)


def send(values, perm):
    arrived = lax.ppermute(encode(values), "batch", perm)
    return decode(with_layout_constraint(arrived, Layout((0, 1))), values.shape)


def reduce_over_batch(columns):
    count = lax.axis_size("batch")
    outer = count // 2
    me = lax.axis_index("batch")
    x = me % 2
    z = me // 2
    pairs = [(i, i ^ 1) for i in range(count)]
    blocks = columns.reshape(outer, 2, -1, columns.shape[1])
    mine = lax.dynamic_index_in_dim(blocks, x, axis=1, keepdims=False)
    theirs = lax.dynamic_index_in_dim(blocks, 1 - x, axis=1, keepdims=False)
    summed = with_layout_constraint(mine + send(theirs, pairs), Layout((0, 1, 2)))
    packets = jnp.stack([encode(summed[j]) for j in range(outer)])
    packets = with_layout_constraint(packets, Layout((0, 1, 2)))
    groups = [[2 * q + p for q in range(outer)] for p in range(2)]
    swapped = lax.all_to_all(jnp.swapaxes(packets, 1, 2), "batch", 0, 0, axis_index_groups=groups, tiled=True)
    arrived = with_layout_constraint(jnp.swapaxes(swapped, 1, 2), Layout((0, 1, 2)))
    others = jnp.stack([decode(arrived[j], summed.shape[1:]) for j in range(outer)])
    others = jnp.where((jnp.arange(outer) == z)[:, None, None], 0.0, others)
    own = lax.dynamic_index_in_dim(summed, z, axis=0, keepdims=False)
    total = own + jnp.sum(others, axis=0)
    return with_layout_constraint(total, Layout((0, 1))).T


def body(inputs, cotangent, weight):
    middle_offset = KW // 2
    reach = middle_offset * TAP_SPACING
    length = inputs.shape[1]
    in_width = inputs.shape[2]
    values = inputs[0].astype(jnp.float32)
    activation, deriv = gelu_factors(values)
    act = activation.astype(jnp.bfloat16)
    seq_count = lax.axis_size("seq")
    batch_count = lax.axis_size("batch")
    counted = batch_count * inputs.shape[0] * length * seq_count
    factor = 1.0 / math.sqrt(float(counted))
    owned = lax.all_to_all(cotangent, "seq", split_axis=2, concat_axis=1, tiled=True)[0]
    own_rows = owned.shape[1]
    owned_padded = jnp.pad(owned, ((reach, reach), (0, 0)))
    whole_act = lax.all_gather(act[None], "seq", axis=1, tiled=True)[0]
    count = whole_act.shape[0]
    updated = []
    for tap_index in range(KW):
        offset = 0 + (2 * middle_offset - tap_index) * TAP_SPACING
        window = lax.dynamic_slice_in_dim(owned_padded, offset, count, 0)
        updated.append(
            lax.dot_general(
                whole_act, window, (((0,), (0,)), ((), ())), preferred_element_type=jnp.float32
            )
        )
    local_columns = jnp.concatenate(updated, axis=0) * factor
    local_columns = with_layout_constraint(local_columns, Layout((0, 1)))
    local_columns, cotangent, deriv = lax.optimization_barrier((local_columns, cotangent, deriv))
    padded_input = extended_2(cotangent, (("seq", 1),), reach)
    extended = padded_input[0]
    grad_act = jnp.zeros((length, in_width), jnp.float32)
    for tap_index in range(KW):
        window_start = (2 * middle_offset - tap_index) * TAP_SPACING
        window = lax.slice_in_dim(extended, window_start, window_start + length, axis=0)
        grad_act = grad_act + jnp.dot(
            window,
            weight[:, tap_index * in_width : (tap_index + 1) * in_width],
            preferred_element_type=jnp.float32,
        )
    grad_input = (grad_act * deriv).astype(jnp.bfloat16)[None]
    if batch_count == 8:
        grad_weight = reduce_over_batch(local_columns)
    else:
        pieces = local_columns.reshape(batch_count, -1, own_rows)
        swapped = lax.all_to_all(pieces, "batch", split_axis=0, concat_axis=0, tiled=True)
        grad_weight = jnp.sum(swapped, axis=0).T
    return (grad_input, grad_weight)


def solution(mesh):
    placed = (P("batch", "seq", None), P("batch", "seq", None), P())
    return jax.shard_map(
        body,
        mesh=mesh,
        in_specs=placed,
        out_specs=(P("batch", "seq", None), P("seq", "batch")),
        check_vma=False,
    )
```

```python
import math

import jax
import jax.numpy as jnp
from jax import lax
from jax.experimental.layout import Layout, with_layout_constraint
from jax.sharding import PartitionSpec as P

KW = 3
TAP_SPACING = 64
HEADROOM = 12.0
TAG = 16


def extended_2(x, sides, width):
    for axis, dim in sides:
        peers, length = (lax.axis_size(axis), x.shape[dim])
        up = [(i, (i + 1) % peers) for i in range(peers - 1)]
        down = [(j, i) for i, j in up]
        last = lax.slice_in_dim(x, length - width, length, axis=dim)
        first = lax.slice_in_dim(x, 0, width, axis=dim)
        before = lax.ppermute(last, axis, up)
        after = lax.ppermute(first, axis, down)
        x = jnp.concatenate([before, x, after], axis=dim)
    return x


def gelu_factors(values):
    normal_cdf = 0.5 * (1.0 + jax.scipy.special.erf(values / math.sqrt(2.0)))
    density = jnp.exp(-0.5 * values * values) / math.sqrt(2.0 * math.pi)
    return (values * normal_cdf, normal_cdf + values * density)


def encode(values):
    flat = values.reshape(-1, values.shape[-1])
    biggest = jnp.maximum(jnp.max(jnp.abs(flat)), 1e-30)
    exponent = jnp.floor(jnp.log2(biggest))
    scaled = (flat * jnp.exp2(HEADROOM - exponent)).astype(jnp.float16)
    tag = jnp.full((TAG, flat.shape[-1]), exponent, jnp.float16)
    return with_layout_constraint(jnp.concatenate([scaled, tag], axis=0), Layout((0, 1)))


def decode(packed, shape):
    exponent = packed[-TAG, 0].astype(jnp.float32)
    values = packed[:-TAG].astype(jnp.float32) * jnp.exp2(exponent - HEADROOM)
    return values.reshape(shape)


def send(values, perm):
    arrived = lax.ppermute(encode(values), "batch", perm)
    return decode(with_layout_constraint(arrived, Layout((0, 1))), values.shape)


def reduce_over_batch(columns):
    count = lax.axis_size("batch")
    outer = count // 2
    me = lax.axis_index("batch")
    x = me % 2
    z = me // 2
    pairs = [(i, i ^ 1) for i in range(count)]
    blocks = columns.reshape(outer, 2, -1, columns.shape[1])
    mine = lax.dynamic_index_in_dim(blocks, x, axis=1, keepdims=False)
    theirs = lax.dynamic_index_in_dim(blocks, 1 - x, axis=1, keepdims=False)
    summed = with_layout_constraint(mine + send(theirs, pairs), Layout((0, 1, 2)))
    total = lax.dynamic_index_in_dim(summed, z, axis=0, keepdims=False)
    for shift in range(1, outer):
        target = lax.dynamic_index_in_dim(summed, (z + shift) % outer, axis=0, keepdims=False)
        perm = [(2 * q + p, 2 * ((q + shift) % outer) + p) for q in range(outer) for p in range(2)]
        total = total + send(target, perm)
    return with_layout_constraint(total, Layout((0, 1))).T


def body(inputs, cotangent, weight):
    middle_offset = KW // 2
    reach = middle_offset * TAP_SPACING
    length = inputs.shape[1]
    in_width = inputs.shape[2]
    values = inputs[0].astype(jnp.float32)
    activation, deriv = gelu_factors(values)
    act = activation.astype(jnp.bfloat16)
    seq_count = lax.axis_size("seq")
    batch_count = lax.axis_size("batch")
    counted = batch_count * inputs.shape[0] * length * seq_count
    factor = 1.0 / math.sqrt(float(counted))
    channels = cotangent[0].T.reshape(seq_count, -1, length)
    arrived = lax.all_to_all(channels, "seq", 0, 0, tiled=True)
    own_rows = arrived.shape[1]
    owned = jnp.transpose(arrived, (1, 0, 2)).reshape(own_rows, -1)
    whole_act = lax.all_gather(act[None], "seq", axis=1, tiled=True)[0]
    count = whole_act.shape[0]
    act_padded = jnp.pad(whole_act, ((reach, reach), (0, 0)))
    updated = []
    for tap_index in range(KW):
        window = lax.slice_in_dim(act_padded, tap_index * TAP_SPACING, tap_index * TAP_SPACING + count, axis=0)
        updated.append(
            lax.dot_general(
                window, owned, (((0,), (1,)), ((), ())), preferred_element_type=jnp.float32
            )
        )
    local_columns = jnp.concatenate(updated, axis=0) * factor
    local_columns = with_layout_constraint(local_columns, Layout((0, 1)))
    local_columns, cotangent, deriv = lax.optimization_barrier((local_columns, cotangent, deriv))
    padded_input = extended_2(cotangent, (("seq", 1),), reach)
    extended = padded_input[0]
    grad_act = jnp.zeros((length, in_width), jnp.float32)
    for tap_index in range(KW):
        window_start = (2 * middle_offset - tap_index) * TAP_SPACING
        window = lax.slice_in_dim(extended, window_start, window_start + length, axis=0)
        grad_act = grad_act + jnp.dot(
            window,
            weight[:, tap_index * in_width : (tap_index + 1) * in_width],
            preferred_element_type=jnp.float32,
        )
    grad_input = (grad_act * deriv).astype(jnp.bfloat16)[None]
    if batch_count == 8:
        grad_weight = reduce_over_batch(local_columns)
    else:
        pieces = local_columns.reshape(batch_count, -1, own_rows)
        swapped = lax.all_to_all(pieces, "batch", split_axis=0, concat_axis=0, tiled=True)
        grad_weight = jnp.sum(swapped, axis=0).T
    return (grad_input, grad_weight)


def solution(mesh):
    placed = (P("batch", "seq", None), P("batch", "seq", None), P())
    return jax.shard_map(
        body,
        mesh=mesh,
        in_specs=placed,
        out_specs=(P("batch", "seq", None), P("seq", "batch")),
        check_vma=False,
    )
```

```python
import math

import jax
import jax.numpy as jnp
from jax import lax
from jax.experimental.layout import Layout, with_layout_constraint
from jax.sharding import PartitionSpec as P

KW = 3
TAP_SPACING = 64
HEADROOM = 12.0
TAG = 16


def extended_2(x, sides, width):
    for axis, dim in sides:
        peers, length = (lax.axis_size(axis), x.shape[dim])
        up = [(i, (i + 1) % peers) for i in range(peers - 1)]
        down = [(j, i) for i, j in up]
        last = lax.slice_in_dim(x, length - width, length, axis=dim)
        first = lax.slice_in_dim(x, 0, width, axis=dim)
        before = lax.ppermute(last, axis, up)
        after = lax.ppermute(first, axis, down)
        x = jnp.concatenate([before, x, after], axis=dim)
    return x


def gelu_factors(values):
    normal_cdf = 0.5 * (1.0 + jax.scipy.special.erf(values / math.sqrt(2.0)))
    density = jnp.exp(-0.5 * values * values) / math.sqrt(2.0 * math.pi)
    return (values * normal_cdf, normal_cdf + values * density)


def encode(values):
    flat = values.reshape(-1, values.shape[-1])
    biggest = jnp.maximum(jnp.max(jnp.abs(flat)), 1e-30)
    exponent = jnp.floor(jnp.log2(biggest))
    scaled = (flat * jnp.exp2(HEADROOM - exponent)).astype(jnp.float16)
    tag = jnp.full((TAG, flat.shape[-1]), exponent, jnp.float16)
    return with_layout_constraint(jnp.concatenate([scaled, tag], axis=0), Layout((0, 1)))


def decode(packed, shape):
    exponent = packed[-TAG, 0].astype(jnp.float32)
    values = packed[:-TAG].astype(jnp.float32) * jnp.exp2(exponent - HEADROOM)
    return values.reshape(shape)


def send(values, perm):
    arrived = lax.ppermute(encode(values), "batch", perm)
    return decode(with_layout_constraint(arrived, Layout((0, 1))), values.shape)


def reduce_over_batch(columns):
    count = lax.axis_size("batch")
    outer = count // 2
    me = lax.axis_index("batch")
    x = me % 2
    z = me // 2
    pairs = [(i, i ^ 1) for i in range(count)]
    blocks = columns.reshape(outer, 2, -1, columns.shape[1])
    mine = lax.dynamic_index_in_dim(blocks, x, axis=1, keepdims=False)
    theirs = lax.dynamic_index_in_dim(blocks, 1 - x, axis=1, keepdims=False)
    summed = with_layout_constraint(mine + send(theirs, pairs), Layout((0, 1, 2)))
    total = lax.dynamic_index_in_dim(summed, z, axis=0, keepdims=False)
    for shift in sorted(range(1, outer), key=lambda d: (min(d, outer - d), -d)):
        target = lax.dynamic_index_in_dim(summed, (z + shift) % outer, axis=0, keepdims=False)
        perm = [(2 * q + p, 2 * ((q + shift) % outer) + p) for q in range(outer) for p in range(2)]
        total = total + send(target, perm)
    return with_layout_constraint(total, Layout((0, 1))).T


def body(inputs, cotangent, weight):
    middle_offset = KW // 2
    reach = middle_offset * TAP_SPACING
    length = inputs.shape[1]
    in_width = inputs.shape[2]
    values = inputs[0].astype(jnp.float32)
    activation, deriv = gelu_factors(values)
    act = activation.astype(jnp.bfloat16)
    seq_count = lax.axis_size("seq")
    batch_count = lax.axis_size("batch")
    counted = batch_count * inputs.shape[0] * length * seq_count
    factor = 1.0 / math.sqrt(float(counted))
    channels = cotangent[0].T.reshape(seq_count, -1, length)
    arrived = lax.all_to_all(channels, "seq", 0, 0, tiled=True)
    own_rows = arrived.shape[1]
    owned = jnp.transpose(arrived, (1, 0, 2)).reshape(own_rows, -1)
    whole_act = lax.all_gather(act[None], "seq", axis=1, tiled=True)[0]
    count = whole_act.shape[0]
    act_padded = jnp.pad(whole_act, ((reach, reach), (0, 0)))
    updated = []
    for tap_index in range(KW):
        window = lax.slice_in_dim(act_padded, tap_index * TAP_SPACING, tap_index * TAP_SPACING + count, axis=0)
        updated.append(
            lax.dot_general(
                window, owned, (((0,), (1,)), ((), ())), preferred_element_type=jnp.float32
            )
        )
    local_columns = jnp.concatenate(updated, axis=0) * factor
    local_columns = with_layout_constraint(local_columns, Layout((0, 1)))
    local_columns, cotangent, deriv = lax.optimization_barrier((local_columns, cotangent, deriv))
    padded_input = extended_2(cotangent, (("seq", 1),), reach)
    extended = padded_input[0]
    grad_act = jnp.zeros((length, in_width), jnp.float32)
    for tap_index in range(KW):
        window_start = (2 * middle_offset - tap_index) * TAP_SPACING
        window = lax.slice_in_dim(extended, window_start, window_start + length, axis=0)
        grad_act = grad_act + jnp.dot(
            window,
            weight[:, tap_index * in_width : (tap_index + 1) * in_width],
            preferred_element_type=jnp.float32,
        )
    grad_input = (grad_act * deriv).astype(jnp.bfloat16)[None]
    if batch_count == 8:
        grad_weight = reduce_over_batch(local_columns)
    else:
        pieces = local_columns.reshape(batch_count, -1, own_rows)
        swapped = lax.all_to_all(pieces, "batch", split_axis=0, concat_axis=0, tiled=True)
        grad_weight = jnp.sum(swapped, axis=0).T
    return (grad_input, grad_weight)


def solution(mesh):
    placed = (P("batch", "seq", None), P("batch", "seq", None), P())
    return jax.shard_map(
        body,
        mesh=mesh,
        in_specs=placed,
        out_specs=(P("batch", "seq", None), P("seq", "batch")),
        check_vma=False,
    )
```

```python
import math

import jax
import jax.numpy as jnp
from jax import lax
from jax.experimental.layout import Layout, with_layout_constraint
from jax.sharding import PartitionSpec as P

KW = 3
TAP_SPACING = 64
HEADROOM = 12.0
TAG = 16


def extended_2(x, sides, width):
    for axis, dim in sides:
        peers, length = (lax.axis_size(axis), x.shape[dim])
        up = [(i, (i + 1) % peers) for i in range(peers - 1)]
        down = [(j, i) for i, j in up]
        last = lax.slice_in_dim(x, length - width, length, axis=dim)
        first = lax.slice_in_dim(x, 0, width, axis=dim)
        before = lax.ppermute(last, axis, up)
        after = lax.ppermute(first, axis, down)
        x = jnp.concatenate([before, x, after], axis=dim)
    return x


def gelu_factors(values):
    normal_cdf = 0.5 * (1.0 + jax.scipy.special.erf(values / math.sqrt(2.0)))
    density = jnp.exp(-0.5 * values * values) / math.sqrt(2.0 * math.pi)
    return (values * normal_cdf, normal_cdf + values * density)


def exponent_of(values):
    flat = values.reshape(-1, values.shape[-1])
    biggest = jnp.max(jnp.max(jnp.abs(flat), axis=0, keepdims=True), axis=1, keepdims=True)
    return jnp.floor(jnp.log2(jnp.maximum(biggest, 1e-30)))


def encode(values, exponent):
    flat = values.reshape(-1, values.shape[-1])
    scaled = (flat * jnp.exp2(HEADROOM - exponent)).astype(jnp.float16)
    tag = jnp.broadcast_to(exponent.astype(jnp.float16), (TAG, flat.shape[-1]))
    return with_layout_constraint(jnp.concatenate([scaled, tag], axis=0), Layout((0, 1)))


def decode(packed, shape):
    exponent = packed[-TAG:1 - TAG, 0:1].astype(jnp.float32)
    values = packed[:-TAG].astype(jnp.float32) * jnp.exp2(exponent - HEADROOM)
    return values.reshape(shape)


def send(values, perm, exponent):
    arrived = lax.ppermute(encode(values, exponent), "batch", perm)
    return decode(with_layout_constraint(arrived, Layout((0, 1))), values.shape)


def reduce_over_batch(columns):
    count = lax.axis_size("batch")
    outer = count // 2
    me = lax.axis_index("batch")
    x = me % 2
    z = me // 2
    pairs = [(i, i ^ 1) for i in range(count)]
    blocks = columns.reshape(outer, 2, -1, columns.shape[1])
    mine = lax.dynamic_index_in_dim(blocks, x, axis=1, keepdims=False)
    theirs = lax.dynamic_index_in_dim(blocks, 1 - x, axis=1, keepdims=False)
    summed = with_layout_constraint(mine + send(theirs, pairs, exponent_of(theirs)), Layout((0, 1, 2)))
    spread = exponent_of(summed)
    total = lax.dynamic_index_in_dim(summed, z, axis=0, keepdims=False)
    for shift in sorted(range(1, outer), key=lambda d: (min(d, outer - d), -d)):
        target = lax.dynamic_index_in_dim(summed, (z + shift) % outer, axis=0, keepdims=False)
        perm = [(2 * q + p, 2 * ((q + shift) % outer) + p) for q in range(outer) for p in range(2)]
        total = total + send(target, perm, spread)
    return with_layout_constraint(total, Layout((0, 1))).T


def body(inputs, cotangent, weight):
    middle_offset = KW // 2
    reach = middle_offset * TAP_SPACING
    length = inputs.shape[1]
    in_width = inputs.shape[2]
    values = inputs[0].astype(jnp.float32)
    activation, deriv = gelu_factors(values)
    act = activation.astype(jnp.bfloat16)
    seq_count = lax.axis_size("seq")
    batch_count = lax.axis_size("batch")
    counted = batch_count * inputs.shape[0] * length * seq_count
    factor = 1.0 / math.sqrt(float(counted))
    channels = cotangent[0].T.reshape(seq_count, -1, length)
    arrived = lax.all_to_all(channels, "seq", 0, 0, tiled=True)
    own_rows = arrived.shape[1]
    owned = jnp.transpose(arrived, (1, 0, 2)).reshape(own_rows, -1)
    whole_act = lax.all_gather(act[None], "seq", axis=1, tiled=True)[0]
    count = whole_act.shape[0]
    act_padded = jnp.pad(whole_act, ((reach, reach), (0, 0)))
    updated = []
    for tap_index in range(KW):
        window = lax.slice_in_dim(act_padded, tap_index * TAP_SPACING, tap_index * TAP_SPACING + count, axis=0)
        updated.append(
            lax.dot_general(
                window, owned, (((0,), (1,)), ((), ())), preferred_element_type=jnp.float32
            )
        )
    local_columns = jnp.concatenate(updated, axis=0) * factor
    local_columns = with_layout_constraint(local_columns, Layout((0, 1)))
    local_columns, cotangent, deriv = lax.optimization_barrier((local_columns, cotangent, deriv))
    padded_input = extended_2(cotangent, (("seq", 1),), reach)
    extended = padded_input[0]
    grad_act = jnp.zeros((length, in_width), jnp.float32)
    for tap_index in range(KW):
        window_start = (2 * middle_offset - tap_index) * TAP_SPACING
        window = lax.slice_in_dim(extended, window_start, window_start + length, axis=0)
        grad_act = grad_act + jnp.dot(
            window,
            weight[:, tap_index * in_width : (tap_index + 1) * in_width],
            preferred_element_type=jnp.float32,
        )
    grad_input = (grad_act * deriv).astype(jnp.bfloat16)[None]
    if batch_count == 8:
        grad_weight = reduce_over_batch(local_columns)
    else:
        pieces = local_columns.reshape(batch_count, -1, own_rows)
        swapped = lax.all_to_all(pieces, "batch", split_axis=0, concat_axis=0, tiled=True)
        grad_weight = jnp.sum(swapped, axis=0).T
    return (grad_input, grad_weight)


def solution(mesh):
    placed = (P("batch", "seq", None), P("batch", "seq", None), P())
    return jax.shard_map(
        body,
        mesh=mesh,
        in_specs=placed,
        out_specs=(P("batch", "seq", None), P("seq", "batch")),
        check_vma=False,
    )
```

```python
import math

import jax
import jax.numpy as jnp
from jax import lax
from jax.experimental.layout import Layout, with_layout_constraint
from jax.sharding import PartitionSpec as P

KW = 3
TAP_SPACING = 64
HEADROOM = 12.0
TAG = 16


def extended_2(x, sides, width):
    for axis, dim in sides:
        peers, length = (lax.axis_size(axis), x.shape[dim])
        up = [(i, (i + 1) % peers) for i in range(peers - 1)]
        down = [(j, i) for i, j in up]
        last = lax.slice_in_dim(x, length - width, length, axis=dim)
        first = lax.slice_in_dim(x, 0, width, axis=dim)
        before = lax.ppermute(last, axis, up)
        after = lax.ppermute(first, axis, down)
        x = jnp.concatenate([before, x, after], axis=dim)
    return x


def gelu_factors(values):
    normal_cdf = 0.5 * (1.0 + jax.scipy.special.erf(values / math.sqrt(2.0)))
    density = jnp.exp(-0.5 * values * values) / math.sqrt(2.0 * math.pi)
    return (values * normal_cdf, normal_cdf + values * density)


def exponent_of(values):
    flat = values.reshape(-1, values.shape[-1])
    biggest = jnp.max(jnp.max(jnp.abs(flat), axis=0, keepdims=True), axis=1, keepdims=True)
    return jnp.floor(jnp.log2(jnp.maximum(biggest, 1e-30)))


def encode(values, exponent):
    flat = values.reshape(-1, values.shape[-1])
    scaled = (flat * jnp.exp2(HEADROOM - exponent)).astype(jnp.float16)
    tag = jnp.broadcast_to(exponent.astype(jnp.float16), (TAG, flat.shape[-1]))
    return with_layout_constraint(jnp.concatenate([scaled, tag], axis=0), Layout((0, 1)))


def decode(packed, shape):
    exponent = packed[-TAG:1 - TAG, 0:1].astype(jnp.float32)
    values = packed[:-TAG].astype(jnp.float32) * jnp.exp2(exponent - HEADROOM)
    return values.reshape(shape), exponent


def send(values, perm, exponent):
    arrived = lax.ppermute(encode(values, exponent), "batch", perm)
    return decode(with_layout_constraint(arrived, Layout((0, 1))), values.shape)


def reduce_over_batch(columns):
    count = lax.axis_size("batch")
    outer = count // 2
    me = lax.axis_index("batch")
    x = me % 2
    z = me // 2
    pairs = [(i, i ^ 1) for i in range(count)]
    blocks = columns.reshape(outer, 2, -1, columns.shape[1])
    mine = lax.dynamic_index_in_dim(blocks, x, axis=1, keepdims=False)
    theirs = lax.dynamic_index_in_dim(blocks, 1 - x, axis=1, keepdims=False)
    received, partner = send(theirs, pairs, exponent_of(theirs))
    summed = with_layout_constraint(mine + received, Layout((0, 1, 2)))
    spread = jnp.maximum(exponent_of(mine), partner) + 1.0
    total = lax.dynamic_index_in_dim(summed, z, axis=0, keepdims=False)
    for shift in sorted(range(1, outer), key=lambda d: (min(d, outer - d), -d)):
        target = lax.dynamic_index_in_dim(summed, (z + shift) % outer, axis=0, keepdims=False)
        perm = [(2 * q + p, 2 * ((q + shift) % outer) + p) for q in range(outer) for p in range(2)]
        total = total + send(target, perm, spread)[0]
    return with_layout_constraint(total, Layout((0, 1))).T


def body(inputs, cotangent, weight):
    middle_offset = KW // 2
    reach = middle_offset * TAP_SPACING
    length = inputs.shape[1]
    in_width = inputs.shape[2]
    values = inputs[0].astype(jnp.float32)
    activation, deriv = gelu_factors(values)
    act = activation.astype(jnp.bfloat16)
    seq_count = lax.axis_size("seq")
    batch_count = lax.axis_size("batch")
    counted = batch_count * inputs.shape[0] * length * seq_count
    factor = 1.0 / math.sqrt(float(counted))
    channels = cotangent[0].T.reshape(seq_count, -1, length)
    arrived = lax.all_to_all(channels, "seq", 0, 0, tiled=True)
    own_rows = arrived.shape[1]
    owned = jnp.transpose(arrived, (1, 0, 2)).reshape(own_rows, -1)
    whole_act = lax.all_gather(act[None], "seq", axis=1, tiled=True)[0]
    count = whole_act.shape[0]
    act_padded = jnp.pad(whole_act, ((reach, reach), (0, 0)))
    updated = []
    for tap_index in range(KW):
        window = lax.slice_in_dim(act_padded, tap_index * TAP_SPACING, tap_index * TAP_SPACING + count, axis=0)
        updated.append(
            lax.dot_general(
                window, owned, (((0,), (1,)), ((), ())), preferred_element_type=jnp.float32
            )
        )
    local_columns = jnp.concatenate(updated, axis=0) * factor
    local_columns = with_layout_constraint(local_columns, Layout((0, 1)))
    local_columns, cotangent, deriv = lax.optimization_barrier((local_columns, cotangent, deriv))
    padded_input = extended_2(cotangent, (("seq", 1),), reach)
    extended = padded_input[0]
    grad_act = jnp.zeros((length, in_width), jnp.float32)
    for tap_index in range(KW):
        window_start = (2 * middle_offset - tap_index) * TAP_SPACING
        window = lax.slice_in_dim(extended, window_start, window_start + length, axis=0)
        grad_act = grad_act + jnp.dot(
            window,
            weight[:, tap_index * in_width : (tap_index + 1) * in_width],
            preferred_element_type=jnp.float32,
        )
    grad_input = (grad_act * deriv).astype(jnp.bfloat16)[None]
    if batch_count == 8:
        grad_weight = reduce_over_batch(local_columns)
    else:
        pieces = local_columns.reshape(batch_count, -1, own_rows)
        swapped = lax.all_to_all(pieces, "batch", split_axis=0, concat_axis=0, tiled=True)
        grad_weight = jnp.sum(swapped, axis=0).T
    return (grad_input, grad_weight)


def solution(mesh):
    placed = (P("batch", "seq", None), P("batch", "seq", None), P())
    return jax.shard_map(
        body,
        mesh=mesh,
        in_specs=placed,
        out_specs=(P("batch", "seq", None), P("seq", "batch")),
        check_vma=False,
    )
```

```python
import math

import jax
import jax.numpy as jnp
from jax import lax
from jax.experimental.layout import Layout, with_layout_constraint
from jax.sharding import PartitionSpec as P

KW = 3
TAP_SPACING = 64
HEADROOM = 12.0
TAG = 16


def extended_2(x, sides, width):
    for axis, dim in sides:
        peers, length = (lax.axis_size(axis), x.shape[dim])
        up = [(i, (i + 1) % peers) for i in range(peers - 1)]
        down = [(j, i) for i, j in up]
        last = lax.slice_in_dim(x, length - width, length, axis=dim)
        first = lax.slice_in_dim(x, 0, width, axis=dim)
        before = lax.ppermute(last, axis, up)
        after = lax.ppermute(first, axis, down)
        x = jnp.concatenate([before, x, after], axis=dim)
    return x


def gelu_factors(values):
    normal_cdf = 0.5 * (1.0 + jax.scipy.special.erf(values / math.sqrt(2.0)))
    density = jnp.exp(-0.5 * values * values) / math.sqrt(2.0 * math.pi)
    return (values * normal_cdf, normal_cdf + values * density)


def exponent_of(values):
    flat = values.reshape(-1, values.shape[-1])
    biggest = jnp.max(jnp.max(jnp.abs(flat), axis=0, keepdims=True), axis=1, keepdims=True)
    return jnp.floor(jnp.log2(jnp.maximum(biggest, 1e-30)))


def encode(values, exponent):
    flat = values.reshape(-1, values.shape[-1])
    scaled = (flat * jnp.exp2(HEADROOM - exponent)).astype(jnp.float16)
    tag = jnp.broadcast_to(exponent.astype(jnp.float16), (TAG, flat.shape[-1]))
    return with_layout_constraint(jnp.concatenate([scaled, tag], axis=0), Layout((0, 1)))


def decode(packed, shape):
    exponent = packed[-TAG:1 - TAG, 0:1].astype(jnp.float32)
    values = packed[:-TAG].astype(jnp.float32) * jnp.exp2(exponent - HEADROOM)
    return values.reshape(shape)


def send(values, perm, exponent):
    arrived = lax.ppermute(encode(values, exponent), "batch", perm)
    return decode(with_layout_constraint(arrived, Layout((0, 1))), values.shape)


def reduce_over_batch(columns):
    count = lax.axis_size("batch")
    outer = count // 2
    me = lax.axis_index("batch")
    x = me % 2
    z = me // 2
    pairs = [(i, i ^ 1) for i in range(count)]
    blocks = columns.reshape(outer, 2, -1, columns.shape[1])
    mine = lax.dynamic_index_in_dim(blocks, x, axis=1, keepdims=False)
    theirs = lax.dynamic_index_in_dim(blocks, 1 - x, axis=1, keepdims=False)
    summed = with_layout_constraint(mine + send(theirs, pairs, exponent_of(theirs)), Layout((0, 1, 2)))
    spread = exponent_of(summed)
    total = lax.dynamic_index_in_dim(summed, z, axis=0, keepdims=False)
    for shift in sorted(range(1, outer), key=lambda d: (min(d, outer - d), -d)):
        target = lax.dynamic_index_in_dim(summed, (z + shift) % outer, axis=0, keepdims=False)
        perm = [(2 * q + p, 2 * ((q + shift) % outer) + p) for q in range(outer) for p in range(2)]
        total = total + send(target, perm, spread)
    return with_layout_constraint(total, Layout((0, 1))).T


def body(inputs, cotangent, weight):
    middle_offset = KW // 2
    reach = middle_offset * TAP_SPACING
    length = inputs.shape[1]
    in_width = inputs.shape[2]
    halo_source = cotangent
    values = inputs[0].astype(jnp.float32)
    activation, deriv = gelu_factors(values)
    act = activation.astype(jnp.bfloat16)
    seq_count = lax.axis_size("seq")
    batch_count = lax.axis_size("batch")
    counted = batch_count * inputs.shape[0] * length * seq_count
    factor = 1.0 / math.sqrt(float(counted))
    channels = cotangent[0].T.reshape(seq_count, -1, length)
    arrived = lax.all_to_all(channels, "seq", 0, 0, tiled=True)
    own_rows = arrived.shape[1]
    owned = jnp.transpose(arrived, (1, 0, 2)).reshape(own_rows, -1)
    whole_act = lax.all_gather(act[None], "seq", axis=1, tiled=True)[0]
    count = whole_act.shape[0]
    act_padded = jnp.pad(whole_act, ((reach, reach), (0, 0)))
    updated = []
    for tap_index in range(KW):
        window = lax.slice_in_dim(act_padded, tap_index * TAP_SPACING, tap_index * TAP_SPACING + count, axis=0)
        updated.append(
            lax.dot_general(
                window, owned, (((0,), (1,)), ((), ())), preferred_element_type=jnp.float32
            )
        )
    local_columns = jnp.concatenate(updated, axis=0) * factor
    local_columns = with_layout_constraint(local_columns, Layout((0, 1)))
    extended = extended_2(halo_source, (("seq", 1),), reach)[0]
    local_columns, extended, deriv = lax.optimization_barrier((local_columns, extended, deriv))
    grad_act = jnp.zeros((length, in_width), jnp.float32)
    for tap_index in range(KW):
        window_start = (2 * middle_offset - tap_index) * TAP_SPACING
        window = lax.slice_in_dim(extended, window_start, window_start + length, axis=0)
        grad_act = grad_act + jnp.dot(
            window,
            weight[:, tap_index * in_width : (tap_index + 1) * in_width],
            preferred_element_type=jnp.float32,
        )
    grad_input = (grad_act * deriv).astype(jnp.bfloat16)[None]
    if batch_count == 8:
        grad_weight = reduce_over_batch(local_columns)
    else:
        pieces = local_columns.reshape(batch_count, -1, own_rows)
        swapped = lax.all_to_all(pieces, "batch", split_axis=0, concat_axis=0, tiled=True)
        grad_weight = jnp.sum(swapped, axis=0).T
    return (grad_input, grad_weight)


def solution(mesh):
    placed = (P("batch", "seq", None), P("batch", "seq", None), P())
    return jax.shard_map(
        body,
        mesh=mesh,
        in_specs=placed,
        out_specs=(P("batch", "seq", None), P("seq", "batch")),
        check_vma=False,
    )
```

```python
import math

import jax
import jax.numpy as jnp
from jax import lax
from jax.experimental.layout import Layout, with_layout_constraint
from jax.sharding import PartitionSpec as P

KW = 3
TAP_SPACING = 64
HEADROOM = 12.0
TAG = 16


def extended_2(x, sides, width):
    for axis, dim in sides:
        peers, length = (lax.axis_size(axis), x.shape[dim])
        up = [(i, (i + 1) % peers) for i in range(peers - 1)]
        down = [(j, i) for i, j in up]
        last = lax.slice_in_dim(x, length - width, length, axis=dim)
        first = lax.slice_in_dim(x, 0, width, axis=dim)
        before = lax.ppermute(last, axis, up)
        after = lax.ppermute(first, axis, down)
        x = jnp.concatenate([before, x, after], axis=dim)
    return x


def gelu_factors(values):
    normal_cdf = 0.5 * (1.0 + jax.scipy.special.erf(values / math.sqrt(2.0)))
    density = jnp.exp(-0.5 * values * values) / math.sqrt(2.0 * math.pi)
    return (values * normal_cdf, normal_cdf + values * density)


def exponent_of(values):
    flat = values.reshape(-1, values.shape[-1])
    biggest = jnp.max(jnp.max(jnp.abs(flat), axis=0, keepdims=True), axis=1, keepdims=True)
    return jnp.floor(jnp.log2(jnp.maximum(biggest, 1e-30)))


def encode(values, exponent):
    flat = values.reshape(-1, values.shape[-1])
    scaled = (flat * jnp.exp2(HEADROOM - exponent)).astype(jnp.float16)
    tag = jnp.broadcast_to(exponent.astype(jnp.float16), (TAG, flat.shape[-1]))
    return with_layout_constraint(jnp.concatenate([scaled, tag], axis=0), Layout((0, 1)))


def decode(packed, shape):
    exponent = packed[-TAG:1 - TAG, 0:1].astype(jnp.float32)
    values = packed[:-TAG].astype(jnp.float32) * jnp.exp2(exponent - HEADROOM)
    return values.reshape(shape), exponent


def send(values, perm, exponent):
    arrived = lax.ppermute(encode(values, exponent), "batch", perm)
    return decode(with_layout_constraint(arrived, Layout((0, 1))), values.shape)


def reduce_over_batch(columns):
    count = lax.axis_size("batch")
    outer = count // 2
    me = lax.axis_index("batch")
    x = me % 2
    z = me // 2
    pairs = [(i, i ^ 1) for i in range(count)]
    blocks = columns.reshape(outer, 2, -1, columns.shape[1])
    mine = lax.dynamic_index_in_dim(blocks, x, axis=1, keepdims=False)
    theirs = lax.dynamic_index_in_dim(blocks, 1 - x, axis=1, keepdims=False)
    received, partner = send(theirs, pairs, exponent_of(theirs))
    summed = with_layout_constraint(mine + received, Layout((0, 1, 2)))
    spread = jnp.maximum(exponent_of(mine), partner) + 1.0
    total = lax.dynamic_index_in_dim(summed, z, axis=0, keepdims=False)
    for shift in sorted(range(1, outer), key=lambda d: (min(d, outer - d), -d)):
        target = lax.dynamic_index_in_dim(summed, (z + shift) % outer, axis=0, keepdims=False)
        perm = [(2 * q + p, 2 * ((q + shift) % outer) + p) for q in range(outer) for p in range(2)]
        total = total + send(target, perm, spread)[0]
    return with_layout_constraint(total, Layout((0, 1))).T


def body(inputs, cotangent, weight):
    middle_offset = KW // 2
    reach = middle_offset * TAP_SPACING
    length = inputs.shape[1]
    in_width = inputs.shape[2]
    halo_source = cotangent
    values = inputs[0].astype(jnp.float32)
    activation, deriv = gelu_factors(values)
    act = activation.astype(jnp.bfloat16)
    seq_count = lax.axis_size("seq")
    batch_count = lax.axis_size("batch")
    counted = batch_count * inputs.shape[0] * length * seq_count
    factor = 1.0 / math.sqrt(float(counted))
    channels = cotangent[0].T.reshape(seq_count, -1, length)
    arrived = lax.all_to_all(channels, "seq", 0, 0, tiled=True)
    own_rows = arrived.shape[1]
    owned = jnp.transpose(arrived, (1, 0, 2)).reshape(own_rows, -1)
    whole_act = lax.all_gather(act[None], "seq", axis=1, tiled=True)[0]
    count = whole_act.shape[0]
    act_padded = jnp.pad(whole_act, ((reach, reach), (0, 0)))
    updated = []
    for tap_index in range(KW):
        window = lax.slice_in_dim(act_padded, tap_index * TAP_SPACING, tap_index * TAP_SPACING + count, axis=0)
        updated.append(
            lax.dot_general(
                window, owned, (((0,), (1,)), ((), ())), preferred_element_type=jnp.float32
            )
        )
    local_columns = jnp.concatenate(updated, axis=0) * factor
    local_columns = with_layout_constraint(local_columns, Layout((0, 1)))
    extended = extended_2(halo_source, (("seq", 1),), reach)[0]
    local_columns, extended, deriv = lax.optimization_barrier((local_columns, extended, deriv))
    grad_act = jnp.zeros((length, in_width), jnp.float32)
    for tap_index in range(KW):
        window_start = (2 * middle_offset - tap_index) * TAP_SPACING
        window = lax.slice_in_dim(extended, window_start, window_start + length, axis=0)
        grad_act = grad_act + jnp.dot(
            window,
            weight[:, tap_index * in_width : (tap_index + 1) * in_width],
            preferred_element_type=jnp.float32,
        )
    grad_input = (grad_act * deriv).astype(jnp.bfloat16)[None]
    if batch_count == 8:
        grad_weight = reduce_over_batch(local_columns)
    else:
        pieces = local_columns.reshape(batch_count, -1, own_rows)
        swapped = lax.all_to_all(pieces, "batch", split_axis=0, concat_axis=0, tiled=True)
        grad_weight = jnp.sum(swapped, axis=0).T
    return (grad_input, grad_weight)


def solution(mesh):
    placed = (P("batch", "seq", None), P("batch", "seq", None), P())
    return jax.shard_map(
        body,
        mesh=mesh,
        in_specs=placed,
        out_specs=(P("batch", "seq", None), P("seq", "batch")),
        check_vma=False,
    )
```

```python
import math

import jax
import jax.numpy as jnp
from jax import lax
from jax.experimental.layout import Layout, with_layout_constraint
from jax.sharding import PartitionSpec as P

KW = 3
TAP_SPACING = 64
HEADROOM = 12.0
TAG = 16


def extended_2(x, sides, width):
    for axis, dim in sides:
        peers, length = (lax.axis_size(axis), x.shape[dim])
        up = [(i, (i + 1) % peers) for i in range(peers - 1)]
        down = [(j, i) for i, j in up]
        last = lax.slice_in_dim(x, length - width, length, axis=dim)
        first = lax.slice_in_dim(x, 0, width, axis=dim)
        before = lax.ppermute(last, axis, up)
        after = lax.ppermute(first, axis, down)
        x = jnp.concatenate([before, x, after], axis=dim)
    return x


def gelu_factors(values):
    normal_cdf = 0.5 * (1.0 + jax.scipy.special.erf(values / math.sqrt(2.0)))
    density = jnp.exp(-0.5 * values * values) / math.sqrt(2.0 * math.pi)
    return (values * normal_cdf, normal_cdf + values * density)


def exponent_of(values):
    flat = values.reshape(-1, values.shape[-1])
    biggest = jnp.max(jnp.max(jnp.abs(flat), axis=0, keepdims=True), axis=1, keepdims=True)
    return jnp.floor(jnp.log2(jnp.maximum(biggest, 1e-30)))


def encode(values, exponent):
    flat = values.reshape(-1, values.shape[-1])
    scaled = (flat * jnp.exp2(HEADROOM - exponent)).astype(jnp.float16)
    tag = jnp.broadcast_to(exponent.astype(jnp.float16), (TAG, flat.shape[-1]))
    return with_layout_constraint(jnp.concatenate([scaled, tag], axis=0), Layout((0, 1)))


def decode(packed, shape):
    exponent = packed[-TAG:1 - TAG, 0:1].astype(jnp.float32)
    values = packed[:-TAG].astype(jnp.float32) * jnp.exp2(exponent - HEADROOM)
    return values.reshape(shape)


def send(values, perm, exponent):
    arrived = lax.ppermute(encode(values, exponent), "batch", perm)
    return decode(with_layout_constraint(arrived, Layout((0, 1))), values.shape)


def reduce_over_batch(columns):
    count = lax.axis_size("batch")
    outer = count // 2
    me = lax.axis_index("batch")
    x = me % 2
    z = me // 2
    pairs = [(i, i ^ 1) for i in range(count)]
    blocks = columns.reshape(outer, 2, -1, columns.shape[1])
    mine = lax.dynamic_index_in_dim(blocks, x, axis=1, keepdims=False)
    theirs = lax.dynamic_index_in_dim(blocks, 1 - x, axis=1, keepdims=False)
    summed = with_layout_constraint(mine + send(theirs, pairs, exponent_of(theirs)), Layout((0, 1, 2)))
    spread = exponent_of(summed)
    total = lax.dynamic_index_in_dim(summed, z, axis=0, keepdims=False)
    for shift in sorted(range(1, outer), key=lambda d: (min(d, outer - d), -d)):
        target = lax.dynamic_index_in_dim(summed, (z + shift) % outer, axis=0, keepdims=False)
        perm = [(2 * q + p, 2 * ((q + shift) % outer) + p) for q in range(outer) for p in range(2)]
        total = total + send(target, perm, spread)
    return with_layout_constraint(total, Layout((0, 1))).T


def gather_over_seq(block):
    count = lax.axis_size("seq")
    me = lax.axis_index("seq")
    bits = count.bit_length() - 1
    if count != 1 << bits:
        return lax.all_gather(block[None], "seq", axis=1, tiled=True)[0]
    stack = block[None]
    for bit in reversed(range(bits)):
        pairs = [(i, i ^ (1 << bit)) for i in range(count)]
        stack = jnp.concatenate([stack, lax.ppermute(stack, "seq", pairs)], axis=0)
    reverse = jnp.array([int(format(v, "0%db" % bits)[::-1], 2) for v in range(count)], jnp.int32)
    order = reverse[jnp.bitwise_xor(me, jnp.arange(count, dtype=jnp.int32))]
    return jnp.take(stack, order, axis=0).reshape(-1, block.shape[-1])


def body(inputs, cotangent, weight):
    middle_offset = KW // 2
    reach = middle_offset * TAP_SPACING
    length = inputs.shape[1]
    in_width = inputs.shape[2]
    halo_source = cotangent
    values = inputs[0].astype(jnp.float32)
    activation, deriv = gelu_factors(values)
    act = activation.astype(jnp.bfloat16)
    seq_count = lax.axis_size("seq")
    batch_count = lax.axis_size("batch")
    counted = batch_count * inputs.shape[0] * length * seq_count
    factor = 1.0 / math.sqrt(float(counted))
    channels = cotangent[0].T.reshape(seq_count, -1, length)
    arrived = lax.all_to_all(channels, "seq", 0, 0, tiled=True)
    own_rows = arrived.shape[1]
    owned = jnp.transpose(arrived, (1, 0, 2)).reshape(own_rows, -1)
    whole_act = gather_over_seq(act)
    count = whole_act.shape[0]
    act_padded = jnp.pad(whole_act, ((reach, reach), (0, 0)))
    updated = []
    for tap_index in range(KW):
        window = lax.slice_in_dim(act_padded, tap_index * TAP_SPACING, tap_index * TAP_SPACING + count, axis=0)
        updated.append(
            lax.dot_general(
                window, owned, (((0,), (1,)), ((), ())), preferred_element_type=jnp.float32
            )
        )
    local_columns = jnp.concatenate(updated, axis=0) * factor
    local_columns = with_layout_constraint(local_columns, Layout((0, 1)))
    extended = extended_2(halo_source, (("seq", 1),), reach)[0]
    local_columns, extended, deriv = lax.optimization_barrier((local_columns, extended, deriv))
    grad_act = jnp.zeros((length, in_width), jnp.float32)
    for tap_index in range(KW):
        window_start = (2 * middle_offset - tap_index) * TAP_SPACING
        window = lax.slice_in_dim(extended, window_start, window_start + length, axis=0)
        grad_act = grad_act + jnp.dot(
            window,
            weight[:, tap_index * in_width : (tap_index + 1) * in_width],
            preferred_element_type=jnp.float32,
        )
    grad_input = (grad_act * deriv).astype(jnp.bfloat16)[None]
    if batch_count == 8:
        grad_weight = reduce_over_batch(local_columns)
    else:
        pieces = local_columns.reshape(batch_count, -1, own_rows)
        swapped = lax.all_to_all(pieces, "batch", split_axis=0, concat_axis=0, tiled=True)
        grad_weight = jnp.sum(swapped, axis=0).T
    return (grad_input, grad_weight)


def solution(mesh):
    placed = (P("batch", "seq", None), P("batch", "seq", None), P())
    return jax.shard_map(
        body,
        mesh=mesh,
        in_specs=placed,
        out_specs=(P("batch", "seq", None), P("seq", "batch")),
        check_vma=False,
    )
```

```python
import math

import jax
import jax.numpy as jnp
from jax import lax
from jax.experimental.layout import Layout, with_layout_constraint
from jax.sharding import PartitionSpec as P

KW = 3
TAP_SPACING = 64
HEADROOM = 12.0
TAG = 16


def extended_2(x, sides, width):
    for axis, dim in sides:
        peers, length = (lax.axis_size(axis), x.shape[dim])
        up = [(i, (i + 1) % peers) for i in range(peers - 1)]
        down = [(j, i) for i, j in up]
        last = lax.slice_in_dim(x, length - width, length, axis=dim)
        first = lax.slice_in_dim(x, 0, width, axis=dim)
        before = lax.ppermute(last, axis, up)
        after = lax.ppermute(first, axis, down)
        x = jnp.concatenate([before, x, after], axis=dim)
    return x


def gelu_factors(values):
    normal_cdf = 0.5 * (1.0 + jax.scipy.special.erf(values / math.sqrt(2.0)))
    density = jnp.exp(-0.5 * values * values) / math.sqrt(2.0 * math.pi)
    return (values * normal_cdf, normal_cdf + values * density)


def exponent_of(values):
    flat = values.reshape(-1, values.shape[-1])
    biggest = jnp.max(jnp.max(jnp.abs(flat), axis=0, keepdims=True), axis=1, keepdims=True)
    return jnp.floor(jnp.log2(jnp.maximum(biggest, 1e-30)))


def encode(values, exponent):
    flat = values.reshape(-1, values.shape[-1])
    scaled = (flat * jnp.exp2(HEADROOM - exponent)).astype(jnp.float16)
    tag = jnp.broadcast_to(exponent.astype(jnp.float16), (TAG, flat.shape[-1]))
    return with_layout_constraint(jnp.concatenate([scaled, tag], axis=0), Layout((0, 1)))


def decode(packed, shape):
    exponent = packed[-TAG:1 - TAG, 0:1].astype(jnp.float32)
    values = packed[:-TAG].astype(jnp.float32) * jnp.exp2(exponent - HEADROOM)
    return values.reshape(shape)


def send(values, perm, exponent):
    arrived = lax.ppermute(encode(values, exponent), "batch", perm)
    return decode(with_layout_constraint(arrived, Layout((0, 1))), values.shape)


def reduce_over_batch(columns):
    count = lax.axis_size("batch")
    outer = count // 2
    me = lax.axis_index("batch")
    x = me % 2
    z = me // 2
    pairs = [(i, i ^ 1) for i in range(count)]
    blocks = columns.reshape(outer, 2, -1, columns.shape[1])
    mine = lax.dynamic_index_in_dim(blocks, x, axis=1, keepdims=False)
    theirs = lax.dynamic_index_in_dim(blocks, 1 - x, axis=1, keepdims=False)
    summed = with_layout_constraint(mine + send(theirs, pairs, exponent_of(theirs)), Layout((0, 1, 2)))
    spread = exponent_of(summed)
    total = lax.dynamic_index_in_dim(summed, z, axis=0, keepdims=False)
    for shift in sorted(range(1, outer), key=lambda d: (min(d, outer - d), -d)):
        target = lax.dynamic_index_in_dim(summed, (z + shift) % outer, axis=0, keepdims=False)
        perm = [(2 * q + p, 2 * ((q + shift) % outer) + p) for q in range(outer) for p in range(2)]
        total = total + send(target, perm, spread)
    return with_layout_constraint(total, Layout((0, 1))).T


def gather_over_seq(block, cot, width):
    count = lax.axis_size("seq")
    me = lax.axis_index("seq")
    bits = count.bit_length() - 1
    rows = cot.shape[0]
    last = cot[rows - width :]
    first = cot[:width]
    odd = me % 2 == 1
    stack = block[None]
    for bit in reversed(range(1, bits)):
        pairs = [(i, i ^ (1 << bit)) for i in range(count)]
        stack = jnp.concatenate([stack, lax.ppermute(stack, "seq", pairs)], axis=0)
    piece = jnp.where(odd, first, last)
    outgoing = jnp.concatenate([stack.reshape(-1, block.shape[-1]), piece], axis=0)
    incoming = lax.ppermute(outgoing, "seq", [(i, i ^ 1) for i in range(count)])
    near = incoming[-width:]
    stack = jnp.concatenate([stack, incoming[:-width].reshape(stack.shape)], axis=0)
    across = [(i, i + 1) for i in range(1, count - 1, 2)] + [(i, i - 1) for i in range(2, count, 2)]
    far = lax.ppermute(jnp.where(odd, last, first), "seq", across)
    before = jnp.where(odd, near, far)
    after = jnp.where(odd, far, near)
    extended = jnp.concatenate([before, cot, after], axis=0)
    reverse = jnp.array([int(format(v, "0%db" % bits)[::-1], 2) for v in range(count)], jnp.int32)
    order = reverse[jnp.bitwise_xor(me, jnp.arange(count, dtype=jnp.int32))]
    return jnp.take(stack, order, axis=0).reshape(-1, block.shape[-1]), extended


def body(inputs, cotangent, weight):
    middle_offset = KW // 2
    reach = middle_offset * TAP_SPACING
    length = inputs.shape[1]
    in_width = inputs.shape[2]
    values = inputs[0].astype(jnp.float32)
    activation, deriv = gelu_factors(values)
    act = activation.astype(jnp.bfloat16)
    seq_count = lax.axis_size("seq")
    batch_count = lax.axis_size("batch")
    counted = batch_count * inputs.shape[0] * length * seq_count
    factor = 1.0 / math.sqrt(float(counted))
    channels = cotangent[0].T.reshape(seq_count, -1, length)
    arrived = lax.all_to_all(channels, "seq", 0, 0, tiled=True)
    own_rows = arrived.shape[1]
    owned = jnp.transpose(arrived, (1, 0, 2)).reshape(own_rows, -1)
    if seq_count >= 2 and seq_count & (seq_count - 1) == 0:
        whole_act, extended = gather_over_seq(act, cotangent[0], reach)
    else:
        whole_act = lax.all_gather(act[None], "seq", axis=1, tiled=True)[0]
        extended = extended_2(cotangent, (("seq", 1),), reach)[0]
    count = whole_act.shape[0]
    act_padded = jnp.pad(whole_act, ((reach, reach), (0, 0)))
    updated = []
    for tap_index in range(KW):
        window = lax.slice_in_dim(act_padded, tap_index * TAP_SPACING, tap_index * TAP_SPACING + count, axis=0)
        updated.append(
            lax.dot_general(
                window, owned, (((0,), (1,)), ((), ())), preferred_element_type=jnp.float32
            )
        )
    local_columns = jnp.concatenate(updated, axis=0) * factor
    local_columns = with_layout_constraint(local_columns, Layout((0, 1)))
    local_columns, extended, deriv = lax.optimization_barrier((local_columns, extended, deriv))
    grad_act = jnp.zeros((length, in_width), jnp.float32)
    for tap_index in range(KW):
        window_start = (2 * middle_offset - tap_index) * TAP_SPACING
        window = lax.slice_in_dim(extended, window_start, window_start + length, axis=0)
        grad_act = grad_act + jnp.dot(
            window,
            weight[:, tap_index * in_width : (tap_index + 1) * in_width],
            preferred_element_type=jnp.float32,
        )
    grad_input = (grad_act * deriv).astype(jnp.bfloat16)[None]
    if batch_count == 8:
        grad_weight = reduce_over_batch(local_columns)
    else:
        pieces = local_columns.reshape(batch_count, -1, own_rows)
        swapped = lax.all_to_all(pieces, "batch", split_axis=0, concat_axis=0, tiled=True)
        grad_weight = jnp.sum(swapped, axis=0).T
    return (grad_input, grad_weight)


def solution(mesh):
    placed = (P("batch", "seq", None), P("batch", "seq", None), P())
    return jax.shard_map(
        body,
        mesh=mesh,
        in_specs=placed,
        out_specs=(P("batch", "seq", None), P("seq", "batch")),
        check_vma=False,
    )
```

```python
import math

import jax
import jax.numpy as jnp
from jax import lax
from jax.experimental.layout import Layout, with_layout_constraint
from jax.sharding import PartitionSpec as P

KW = 3
TAP_SPACING = 64
HEADROOM = 12.0
TAG = 16


def extended_2(x, sides, width):
    for axis, dim in sides:
        peers, length = (lax.axis_size(axis), x.shape[dim])
        up = [(i, (i + 1) % peers) for i in range(peers - 1)]
        down = [(j, i) for i, j in up]
        last = lax.slice_in_dim(x, length - width, length, axis=dim)
        first = lax.slice_in_dim(x, 0, width, axis=dim)
        before = lax.ppermute(last, axis, up)
        after = lax.ppermute(first, axis, down)
        x = jnp.concatenate([before, x, after], axis=dim)
    return x


def gelu_factors(values):
    normal_cdf = 0.5 * (1.0 + jax.scipy.special.erf(values / math.sqrt(2.0)))
    density = jnp.exp(-0.5 * values * values) / math.sqrt(2.0 * math.pi)
    return (values * normal_cdf, normal_cdf + values * density)


def exponent_of(values):
    flat = values.reshape(-1, values.shape[-1])
    biggest = jnp.max(jnp.max(jnp.abs(flat), axis=0, keepdims=True), axis=1, keepdims=True)
    return jnp.floor(jnp.log2(jnp.maximum(biggest, 1e-30)))


def encode(values, exponent):
    flat = values.reshape(-1, values.shape[-1])
    scaled = (flat * jnp.exp2(HEADROOM - exponent)).astype(jnp.float16)
    tag = jnp.broadcast_to(exponent.astype(jnp.float16), (TAG, flat.shape[-1]))
    return with_layout_constraint(jnp.concatenate([scaled, tag], axis=0), Layout((0, 1)))


def decode(packed, shape):
    exponent = packed[-TAG:1 - TAG, 0:1].astype(jnp.float32)
    values = packed[:-TAG].astype(jnp.float32) * jnp.exp2(exponent - HEADROOM)
    return values.reshape(shape)


def send(values, perm, exponent):
    arrived = lax.ppermute(encode(values, exponent), "batch", perm)
    return decode(with_layout_constraint(arrived, Layout((0, 1))), values.shape)


def reduce_over_batch(columns):
    count = lax.axis_size("batch")
    outer = count // 2
    me = lax.axis_index("batch")
    x = me % 2
    z = me // 2
    pairs = [(i, i ^ 1) for i in range(count)]
    blocks = columns.reshape(outer, 2, -1, columns.shape[1])
    mine = lax.dynamic_index_in_dim(blocks, x, axis=1, keepdims=False)
    theirs = lax.dynamic_index_in_dim(blocks, 1 - x, axis=1, keepdims=False)
    summed = with_layout_constraint(mine + send(theirs, pairs, exponent_of(theirs)), Layout((0, 1, 2)))
    spread = exponent_of(summed)
    total = lax.dynamic_index_in_dim(summed, z, axis=0, keepdims=False)
    for shift in sorted(range(1, outer), key=lambda d: (min(d, outer - d), -d)):
        target = lax.dynamic_index_in_dim(summed, (z + shift) % outer, axis=0, keepdims=False)
        perm = [(2 * q + p, 2 * ((q + shift) % outer) + p) for q in range(outer) for p in range(2)]
        total = total + send(target, perm, spread)
    return with_layout_constraint(total, Layout((0, 1))).T


def gather_over_seq(block, cot, width):
    count = lax.axis_size("seq")
    me = lax.axis_index("seq")
    bits = count.bit_length() - 1
    rows = cot.shape[0]
    last = cot[rows - width :]
    first = cot[:width]
    odd = me % 2 == 1
    stack = block[None]
    for bit in reversed(range(1, bits)):
        pairs = [(i, i ^ (1 << bit)) for i in range(count)]
        stack = jnp.concatenate([stack, lax.ppermute(stack, "seq", pairs)], axis=0)
    piece = jnp.where(odd, first, last)
    outgoing = jnp.concatenate([stack.reshape(-1, block.shape[-1]), piece], axis=0)
    incoming = lax.ppermute(outgoing, "seq", [(i, i ^ 1) for i in range(count)])
    near = incoming[-width:]
    stack = jnp.concatenate([stack, incoming[:-width].reshape(stack.shape)], axis=0)
    across = [(i, i + 1) for i in range(1, count - 1, 2)] + [(i, i - 1) for i in range(2, count, 2)]
    far = lax.ppermute(jnp.where(odd, last, first), "seq", across)
    before = jnp.where(odd, near, far)
    after = jnp.where(odd, far, near)
    extended = jnp.concatenate([before, cot, after], axis=0)
    reverse = jnp.array([int(format(v, "0%db" % bits)[::-1], 2) for v in range(count)], jnp.int32)
    order = reverse[jnp.bitwise_xor(me, jnp.arange(count, dtype=jnp.int32))]
    return jnp.take(stack, order, axis=0).reshape(-1, block.shape[-1]), extended


def gather_over_seq4(block, cot, width):
    me = lax.axis_index("seq")
    rows = cot.shape[0]
    last = cot[rows - width :]
    first = cot[:width]
    odd = me % 2 == 1
    flat = lambda a: a.reshape(-1, block.shape[-1])
    outgoing = jnp.concatenate([block, jnp.where(odd, last, first)], axis=0)
    incoming = lax.ppermute(outgoing, "seq", [(i, 3 - i) for i in range(4)])
    far = jnp.where((me == 0) | (me == 3), jnp.zeros_like(first), incoming[-width:])
    stack = jnp.stack([block, incoming[:-width]])
    outgoing = jnp.concatenate([flat(stack), jnp.where(odd, first, last)], axis=0)
    incoming = lax.ppermute(outgoing, "seq", [(i, i ^ 1) for i in range(4)])
    near = incoming[-width:]
    stack = jnp.concatenate([stack, incoming[:-width].reshape(stack.shape)], axis=0)
    before = jnp.where(odd, near, far)
    after = jnp.where(odd, far, near)
    extended = jnp.concatenate([before, cot, after], axis=0)
    partner = jnp.bitwise_xor(me, 1)
    sources = jnp.stack([me, 3 - me, partner, 3 - partner])
    order = jnp.sum(jnp.arange(4)[None, :] * (sources[None, :] == jnp.arange(4)[:, None]), axis=1)
    return flat(jnp.take(stack, order, axis=0)), extended


def body(inputs, cotangent, weight):
    middle_offset = KW // 2
    reach = middle_offset * TAP_SPACING
    length = inputs.shape[1]
    in_width = inputs.shape[2]
    values = inputs[0].astype(jnp.float32)
    activation, deriv = gelu_factors(values)
    act = activation.astype(jnp.bfloat16)
    seq_count = lax.axis_size("seq")
    batch_count = lax.axis_size("batch")
    counted = batch_count * inputs.shape[0] * length * seq_count
    factor = 1.0 / math.sqrt(float(counted))
    channels = cotangent[0].T.reshape(seq_count, -1, length)
    arrived = lax.all_to_all(channels, "seq", 0, 0, tiled=True)
    own_rows = arrived.shape[1]
    owned = jnp.transpose(arrived, (1, 0, 2)).reshape(own_rows, -1)
    if seq_count == 4:
        whole_act, extended = gather_over_seq4(act, cotangent[0], reach)
    elif seq_count >= 2 and seq_count & (seq_count - 1) == 0:
        whole_act, extended = gather_over_seq(act, cotangent[0], reach)
    else:
        whole_act = lax.all_gather(act[None], "seq", axis=1, tiled=True)[0]
        extended = extended_2(cotangent, (("seq", 1),), reach)[0]
    count = whole_act.shape[0]
    act_padded = jnp.pad(whole_act, ((reach, reach), (0, 0)))
    updated = []
    for tap_index in range(KW):
        window = lax.slice_in_dim(act_padded, tap_index * TAP_SPACING, tap_index * TAP_SPACING + count, axis=0)
        updated.append(
            lax.dot_general(
                window, owned, (((0,), (1,)), ((), ())), preferred_element_type=jnp.float32
            )
        )
    local_columns = jnp.concatenate(updated, axis=0) * factor
    local_columns = with_layout_constraint(local_columns, Layout((0, 1)))
    local_columns, extended, deriv = lax.optimization_barrier((local_columns, extended, deriv))
    grad_act = jnp.zeros((length, in_width), jnp.float32)
    for tap_index in range(KW):
        window_start = (2 * middle_offset - tap_index) * TAP_SPACING
        window = lax.slice_in_dim(extended, window_start, window_start + length, axis=0)
        grad_act = grad_act + jnp.dot(
            window,
            weight[:, tap_index * in_width : (tap_index + 1) * in_width],
            preferred_element_type=jnp.float32,
        )
    grad_input = (grad_act * deriv).astype(jnp.bfloat16)[None]
    if batch_count == 8:
        grad_weight = reduce_over_batch(local_columns)
    else:
        pieces = local_columns.reshape(batch_count, -1, own_rows)
        swapped = lax.all_to_all(pieces, "batch", split_axis=0, concat_axis=0, tiled=True)
        grad_weight = jnp.sum(swapped, axis=0).T
    return (grad_input, grad_weight)


def solution(mesh):
    placed = (P("batch", "seq", None), P("batch", "seq", None), P())
    return jax.shard_map(
        body,
        mesh=mesh,
        in_specs=placed,
        out_specs=(P("batch", "seq", None), P("seq", "batch")),
        check_vma=False,
    )
```

```python
import math

import jax
import jax.numpy as jnp
from jax import lax
from jax.experimental.layout import Layout, with_layout_constraint
from jax.sharding import PartitionSpec as P

KW = 3
TAP_SPACING = 64
HEADROOM = 12.0
TAG = 16


def extended_2(x, sides, width):
    for axis, dim in sides:
        peers, length = (lax.axis_size(axis), x.shape[dim])
        up = [(i, (i + 1) % peers) for i in range(peers - 1)]
        down = [(j, i) for i, j in up]
        last = lax.slice_in_dim(x, length - width, length, axis=dim)
        first = lax.slice_in_dim(x, 0, width, axis=dim)
        before = lax.ppermute(last, axis, up)
        after = lax.ppermute(first, axis, down)
        x = jnp.concatenate([before, x, after], axis=dim)
    return x


def gelu_factors(values):
    normal_cdf = 0.5 * (1.0 + jax.scipy.special.erf(values / math.sqrt(2.0)))
    density = jnp.exp(-0.5 * values * values) / math.sqrt(2.0 * math.pi)
    return (values * normal_cdf, normal_cdf + values * density)


def exponent_of(values):
    flat = values.reshape(-1, values.shape[-1])
    biggest = jnp.max(jnp.max(jnp.abs(flat), axis=0, keepdims=True), axis=1, keepdims=True)
    return jnp.floor(jnp.log2(jnp.maximum(biggest, 1e-30)))


def encode(values, exponent):
    flat = values.reshape(-1, values.shape[-1])
    scaled = (flat * jnp.exp2(HEADROOM - exponent)).astype(jnp.float16)
    tag = jnp.broadcast_to(exponent.astype(jnp.float16), (TAG, flat.shape[-1]))
    return with_layout_constraint(jnp.concatenate([scaled, tag], axis=0), Layout((0, 1)))


def decode(packed, shape):
    exponent = packed[-TAG:1 - TAG, 0:1].astype(jnp.float32)
    values = packed[:-TAG].astype(jnp.float32) * jnp.exp2(exponent - HEADROOM)
    return values.reshape(shape)


def send(values, perm, exponent):
    arrived = lax.ppermute(encode(values, exponent), "batch", perm)
    return decode(with_layout_constraint(arrived, Layout((0, 1))), values.shape)


def reduce_over_batch(columns):
    count = lax.axis_size("batch")
    outer = count // 2
    me = lax.axis_index("batch")
    x = me % 2
    z = me // 2
    pairs = [(i, i ^ 1) for i in range(count)]
    blocks = columns.reshape(outer, 2, -1, columns.shape[1])
    mine = lax.dynamic_index_in_dim(blocks, x, axis=1, keepdims=False)
    theirs = lax.dynamic_index_in_dim(blocks, 1 - x, axis=1, keepdims=False)
    summed = with_layout_constraint(mine + send(theirs, pairs, exponent_of(theirs)), Layout((0, 1, 2)))
    spread = exponent_of(summed)
    total = lax.dynamic_index_in_dim(summed, z, axis=0, keepdims=False)
    for shift in sorted(range(1, outer), key=lambda d: (min(d, outer - d), -d)):
        target = lax.dynamic_index_in_dim(summed, (z + shift) % outer, axis=0, keepdims=False)
        perm = [(2 * q + p, 2 * ((q + shift) % outer) + p) for q in range(outer) for p in range(2)]
        total = total + send(target, perm, spread)
    return with_layout_constraint(total, Layout((0, 1))).T


def gather_over_seq(block, cot, width):
    count = lax.axis_size("seq")
    me = lax.axis_index("seq")
    bits = count.bit_length() - 1
    rows = cot.shape[0]
    last = cot[rows - width :]
    first = cot[:width]
    odd = me % 2 == 1
    stack = block[None]
    for bit in reversed(range(1, bits)):
        pairs = [(i, i ^ (1 << bit)) for i in range(count)]
        stack = jnp.concatenate([stack, lax.ppermute(stack, "seq", pairs)], axis=0)
    piece = jnp.where(odd, first, last)
    outgoing = jnp.concatenate([stack.reshape(-1, block.shape[-1]), piece], axis=0)
    incoming = lax.ppermute(outgoing, "seq", [(i, i ^ 1) for i in range(count)])
    near = incoming[-width:]
    stack = jnp.concatenate([stack, incoming[:-width].reshape(stack.shape)], axis=0)
    across = [(i, i + 1) for i in range(1, count - 1, 2)] + [(i, i - 1) for i in range(2, count, 2)]
    far = lax.ppermute(jnp.where(odd, last, first), "seq", across)
    before = jnp.where(odd, near, far)
    after = jnp.where(odd, far, near)
    extended = jnp.concatenate([before, cot, after], axis=0)
    reverse = jnp.array([int(format(v, "0%db" % bits)[::-1], 2) for v in range(count)], jnp.int32)
    order = reverse[jnp.bitwise_xor(me, jnp.arange(count, dtype=jnp.int32))]
    return jnp.take(stack, order, axis=0).reshape(-1, block.shape[-1]), extended


def exchange_over_seq4(block, cot, channels, width):
    me = lax.axis_index("seq")
    rows = cot.shape[0]
    last = cot[rows - width :]
    first = cot[:width]
    odd = me % 2 == 1
    lanes = block.shape[-1]
    flat = lambda a: a.reshape(-1, lanes)
    pick = lambda j: lax.dynamic_index_in_dim(channels, j, axis=0, keepdims=False)
    outgoing = jnp.stack([pick(me ^ 2), pick(me ^ 3)])
    payload = jnp.concatenate([block, flat(outgoing)], axis=0)
    incoming = lax.ppermute(payload, "seq", [(i, i ^ 2) for i in range(4)])
    stack = jnp.stack([block, incoming[:rows]])
    first_items = incoming[rows:].reshape(outgoing.shape)
    outgoing = jnp.stack([pick(me ^ 1), first_items[1]])
    piece = jnp.where(odd, first, last)
    payload = jnp.concatenate([flat(stack), flat(outgoing), piece], axis=0)
    incoming = lax.ppermute(payload, "seq", [(i, i ^ 1) for i in range(4)])
    near = incoming[-width:]
    stack = jnp.concatenate([stack, incoming[: 2 * rows].reshape(stack.shape)], axis=0)
    second_items = incoming[2 * rows : -width].reshape(outgoing.shape)
    across = [(1, 2), (2, 1)]
    far = lax.ppermute(jnp.where(odd, last, first), "seq", across)
    before = jnp.where(odd, near, far)
    after = jnp.where(odd, far, near)
    extended = jnp.concatenate([before, cot, after], axis=0)
    items = jnp.stack([pick(me), first_items[0], second_items[0], second_items[1]])
    reverse = jnp.array([0, 2, 1, 3], jnp.int32)
    order = reverse[jnp.bitwise_xor(me, jnp.arange(4, dtype=jnp.int32))]
    whole = flat(jnp.take(stack, order, axis=0))
    owned = jnp.take(items, order, axis=0)
    return whole, extended, jnp.transpose(owned, (1, 0, 2)).reshape(owned.shape[1], -1)


def body(inputs, cotangent, weight):
    middle_offset = KW // 2
    reach = middle_offset * TAP_SPACING
    length = inputs.shape[1]
    in_width = inputs.shape[2]
    values = inputs[0].astype(jnp.float32)
    activation, deriv = gelu_factors(values)
    act = activation.astype(jnp.bfloat16)
    seq_count = lax.axis_size("seq")
    batch_count = lax.axis_size("batch")
    counted = batch_count * inputs.shape[0] * length * seq_count
    factor = 1.0 / math.sqrt(float(counted))
    channels = cotangent[0].T.reshape(seq_count, -1, length)
    own_rows = channels.shape[1]
    if seq_count == 4:
        whole_act, extended, owned = exchange_over_seq4(act, cotangent[0], channels, reach)
    else:
        arrived = lax.all_to_all(channels, "seq", 0, 0, tiled=True)
        owned = jnp.transpose(arrived, (1, 0, 2)).reshape(own_rows, -1)
        if seq_count >= 2 and seq_count & (seq_count - 1) == 0:
            whole_act, extended = gather_over_seq(act, cotangent[0], reach)
        else:
            whole_act = lax.all_gather(act[None], "seq", axis=1, tiled=True)[0]
            extended = extended_2(cotangent, (("seq", 1),), reach)[0]
    count = whole_act.shape[0]
    act_padded = jnp.pad(whole_act, ((reach, reach), (0, 0)))
    updated = []
    for tap_index in range(KW):
        window = lax.slice_in_dim(act_padded, tap_index * TAP_SPACING, tap_index * TAP_SPACING + count, axis=0)
        updated.append(
            lax.dot_general(
                window, owned, (((0,), (1,)), ((), ())), preferred_element_type=jnp.float32
            )
        )
    local_columns = jnp.concatenate(updated, axis=0) * factor
    local_columns = with_layout_constraint(local_columns, Layout((0, 1)))
    local_columns, extended, deriv = lax.optimization_barrier((local_columns, extended, deriv))
    grad_act = jnp.zeros((length, in_width), jnp.float32)
    for tap_index in range(KW):
        window_start = (2 * middle_offset - tap_index) * TAP_SPACING
        window = lax.slice_in_dim(extended, window_start, window_start + length, axis=0)
        grad_act = grad_act + jnp.dot(
            window,
            weight[:, tap_index * in_width : (tap_index + 1) * in_width],
            preferred_element_type=jnp.float32,
        )
    grad_input = (grad_act * deriv).astype(jnp.bfloat16)[None]
    if batch_count == 8:
        grad_weight = reduce_over_batch(local_columns)
    else:
        pieces = local_columns.reshape(batch_count, -1, own_rows)
        swapped = lax.all_to_all(pieces, "batch", split_axis=0, concat_axis=0, tiled=True)
        grad_weight = jnp.sum(swapped, axis=0).T
    return (grad_input, grad_weight)


def solution(mesh):
    placed = (P("batch", "seq", None), P("batch", "seq", None), P())
    return jax.shard_map(
        body,
        mesh=mesh,
        in_specs=placed,
        out_specs=(P("batch", "seq", None), P("seq", "batch")),
        check_vma=False,
    )
```

```python
import math

import jax
import jax.numpy as jnp
from jax import lax
from jax.experimental.layout import Layout, with_layout_constraint
from jax.sharding import PartitionSpec as P

KW = 3
TAP_SPACING = 64
HEADROOM = 12.0
TAG = 16


def extended_2(x, sides, width):
    for axis, dim in sides:
        peers, length = (lax.axis_size(axis), x.shape[dim])
        up = [(i, (i + 1) % peers) for i in range(peers - 1)]
        down = [(j, i) for i, j in up]
        last = lax.slice_in_dim(x, length - width, length, axis=dim)
        first = lax.slice_in_dim(x, 0, width, axis=dim)
        before = lax.ppermute(last, axis, up)
        after = lax.ppermute(first, axis, down)
        x = jnp.concatenate([before, x, after], axis=dim)
    return x


def gelu_factors(values):
    normal_cdf = 0.5 * (1.0 + jax.scipy.special.erf(values / math.sqrt(2.0)))
    density = jnp.exp(-0.5 * values * values) / math.sqrt(2.0 * math.pi)
    return (values * normal_cdf, normal_cdf + values * density)


def exponent_of(values):
    flat = values.reshape(-1, values.shape[-1])
    biggest = jnp.max(jnp.max(jnp.abs(flat), axis=0, keepdims=True), axis=1, keepdims=True)
    return jnp.floor(jnp.log2(jnp.maximum(biggest, 1e-30)))


def encode(values, exponent):
    flat = values.reshape(-1, values.shape[-1])
    scaled = (flat * jnp.exp2(HEADROOM - exponent)).astype(jnp.float16)
    tag = jnp.broadcast_to(exponent.astype(jnp.float16), (TAG, flat.shape[-1]))
    return with_layout_constraint(jnp.concatenate([scaled, tag], axis=0), Layout((0, 1)))


def decode(packed, shape):
    exponent = packed[-TAG:1 - TAG, 0:1].astype(jnp.float32)
    values = packed[:-TAG].astype(jnp.float32) * jnp.exp2(exponent - HEADROOM)
    return values.reshape(shape)


def send(values, perm, exponent):
    arrived = lax.ppermute(encode(values, exponent), "batch", perm)
    return decode(with_layout_constraint(arrived, Layout((0, 1))), values.shape)


def reduce_over_batch(columns):
    count = lax.axis_size("batch")
    outer = count // 2
    me = lax.axis_index("batch")
    x = me % 2
    z = me // 2
    pairs = [(i, i ^ 1) for i in range(count)]
    blocks = columns.reshape(outer, 2, -1, columns.shape[1])
    mine = lax.dynamic_index_in_dim(blocks, x, axis=1, keepdims=False)
    theirs = lax.dynamic_index_in_dim(blocks, 1 - x, axis=1, keepdims=False)
    flipped = jnp.transpose(theirs, (2, 0, 1)).reshape(theirs.shape[2], -1)
    received = send(flipped, pairs, exponent_of(flipped))
    received = jnp.transpose(received.reshape(theirs.shape[2], theirs.shape[0], theirs.shape[1]), (1, 2, 0))
    summed = with_layout_constraint(mine + received, Layout((0, 1, 2)))
    spread = exponent_of(summed)
    total = lax.dynamic_index_in_dim(summed, z, axis=0, keepdims=False)
    for shift in sorted(range(1, outer), key=lambda d: (min(d, outer - d), -d)):
        target = lax.dynamic_index_in_dim(summed, (z + shift) % outer, axis=0, keepdims=False)
        perm = [(2 * q + p, 2 * ((q + shift) % outer) + p) for q in range(outer) for p in range(2)]
        total = total + send(target, perm, spread)
    return with_layout_constraint(total, Layout((0, 1))).T


def gather_over_seq(block, cot, width):
    count = lax.axis_size("seq")
    me = lax.axis_index("seq")
    bits = count.bit_length() - 1
    rows = cot.shape[0]
    last = cot[rows - width :]
    first = cot[:width]
    odd = me % 2 == 1
    stack = block[None]
    for bit in reversed(range(1, bits)):
        pairs = [(i, i ^ (1 << bit)) for i in range(count)]
        stack = jnp.concatenate([stack, lax.ppermute(stack, "seq", pairs)], axis=0)
    piece = jnp.where(odd, first, last)
    outgoing = jnp.concatenate([stack.reshape(-1, block.shape[-1]), piece], axis=0)
    incoming = lax.ppermute(outgoing, "seq", [(i, i ^ 1) for i in range(count)])
    near = incoming[-width:]
    stack = jnp.concatenate([stack, incoming[:-width].reshape(stack.shape)], axis=0)
    across = [(i, i + 1) for i in range(1, count - 1, 2)] + [(i, i - 1) for i in range(2, count, 2)]
    far = lax.ppermute(jnp.where(odd, last, first), "seq", across)
    before = jnp.where(odd, near, far)
    after = jnp.where(odd, far, near)
    extended = jnp.concatenate([before, cot, after], axis=0)
    reverse = jnp.array([int(format(v, "0%db" % bits)[::-1], 2) for v in range(count)], jnp.int32)
    order = reverse[jnp.bitwise_xor(me, jnp.arange(count, dtype=jnp.int32))]
    return jnp.take(stack, order, axis=0).reshape(-1, block.shape[-1]), extended


def body(inputs, cotangent, weight):
    middle_offset = KW // 2
    reach = middle_offset * TAP_SPACING
    length = inputs.shape[1]
    in_width = inputs.shape[2]
    values = inputs[0].astype(jnp.float32)
    activation, deriv = gelu_factors(values)
    act = activation.astype(jnp.bfloat16)
    seq_count = lax.axis_size("seq")
    batch_count = lax.axis_size("batch")
    counted = batch_count * inputs.shape[0] * length * seq_count
    factor = 1.0 / math.sqrt(float(counted))
    channels = cotangent[0].T.reshape(seq_count, -1, length)
    arrived = lax.all_to_all(channels, "seq", 0, 0, tiled=True)
    own_rows = arrived.shape[1]
    owned = jnp.transpose(arrived, (1, 0, 2)).reshape(own_rows, -1)
    if seq_count >= 2 and seq_count & (seq_count - 1) == 0:
        whole_act, extended = gather_over_seq(act, cotangent[0], reach)
    else:
        whole_act = lax.all_gather(act[None], "seq", axis=1, tiled=True)[0]
        extended = extended_2(cotangent, (("seq", 1),), reach)[0]
    count = whole_act.shape[0]
    act_padded = jnp.pad(whole_act, ((reach, reach), (0, 0)))
    updated = []
    for tap_index in range(KW):
        window = lax.slice_in_dim(act_padded, tap_index * TAP_SPACING, tap_index * TAP_SPACING + count, axis=0)
        updated.append(
            lax.dot_general(
                window, owned, (((0,), (1,)), ((), ())), preferred_element_type=jnp.float32
            )
        )
    local_columns = jnp.concatenate(updated, axis=0) * factor
    local_columns = with_layout_constraint(local_columns, Layout((0, 1)))
    local_columns, extended, deriv = lax.optimization_barrier((local_columns, extended, deriv))
    grad_act = jnp.zeros((length, in_width), jnp.float32)
    for tap_index in range(KW):
        window_start = (2 * middle_offset - tap_index) * TAP_SPACING
        window = lax.slice_in_dim(extended, window_start, window_start + length, axis=0)
        grad_act = grad_act + jnp.dot(
            window,
            weight[:, tap_index * in_width : (tap_index + 1) * in_width],
            preferred_element_type=jnp.float32,
        )
    grad_input = (grad_act * deriv).astype(jnp.bfloat16)[None]
    if batch_count == 8:
        grad_weight = reduce_over_batch(local_columns)
    else:
        pieces = local_columns.reshape(batch_count, -1, own_rows)
        swapped = lax.all_to_all(pieces, "batch", split_axis=0, concat_axis=0, tiled=True)
        grad_weight = jnp.sum(swapped, axis=0).T
    return (grad_input, grad_weight)


def solution(mesh):
    placed = (P("batch", "seq", None), P("batch", "seq", None), P())
    return jax.shard_map(
        body,
        mesh=mesh,
        in_specs=placed,
        out_specs=(P("batch", "seq", None), P("seq", "batch")),
        check_vma=False,
    )
```

```python
import math

import jax
import jax.numpy as jnp
from jax import lax
from jax.experimental.layout import Layout, with_layout_constraint
from jax.sharding import PartitionSpec as P

KW = 3
TAP_SPACING = 64
HEADROOM = 12.0
TAG = 16


def extended_2(x, sides, width):
    for axis, dim in sides:
        peers, length = (lax.axis_size(axis), x.shape[dim])
        up = [(i, (i + 1) % peers) for i in range(peers - 1)]
        down = [(j, i) for i, j in up]
        last = lax.slice_in_dim(x, length - width, length, axis=dim)
        first = lax.slice_in_dim(x, 0, width, axis=dim)
        before = lax.ppermute(last, axis, up)
        after = lax.ppermute(first, axis, down)
        x = jnp.concatenate([before, x, after], axis=dim)
    return x


def gelu_factors(values):
    normal_cdf = 0.5 * (1.0 + jax.scipy.special.erf(values / math.sqrt(2.0)))
    density = jnp.exp(-0.5 * values * values) / math.sqrt(2.0 * math.pi)
    return (values * normal_cdf, normal_cdf + values * density)


def exponent_of(values):
    flat = values.reshape(-1, values.shape[-1])
    biggest = jnp.max(jnp.max(jnp.abs(flat), axis=0, keepdims=True), axis=1, keepdims=True)
    return jnp.floor(jnp.log2(jnp.maximum(biggest, 1e-30)))


def encode(values, exponent):
    flat = values.reshape(-1, values.shape[-1])
    scaled = (flat * jnp.exp2(HEADROOM - exponent)).astype(jnp.float16)
    tag = jnp.broadcast_to(exponent.astype(jnp.float16), (TAG, flat.shape[-1]))
    return with_layout_constraint(jnp.concatenate([scaled, tag], axis=0), Layout((0, 1)))


def decode(packed, shape):
    exponent = packed[-TAG:1 - TAG, 0:1].astype(jnp.float32)
    values = packed[:-TAG].astype(jnp.float32) * jnp.exp2(exponent - HEADROOM)
    return values.reshape(shape)


def send(values, perm, exponent):
    arrived = lax.ppermute(encode(values, exponent), "batch", perm)
    return decode(with_layout_constraint(arrived, Layout((0, 1))), values.shape)


def reduce_over_batch(columns):
    count = lax.axis_size("batch")
    outer = count // 2
    me = lax.axis_index("batch")
    x = me % 2
    z = me // 2
    pairs = [(i, i ^ 1) for i in range(count)]
    blocks = columns.reshape(outer, 2, -1, columns.shape[1])
    mine = lax.dynamic_index_in_dim(blocks, x, axis=1, keepdims=False)
    theirs = lax.dynamic_index_in_dim(blocks, 1 - x, axis=1, keepdims=False)
    half = outer // 2
    exponent = exponent_of(theirs)
    received = jnp.concatenate(
        [send(theirs[:half], pairs, exponent), send(theirs[half:], pairs, exponent)], axis=0
    )
    summed = with_layout_constraint(mine + received, Layout((0, 1, 2)))
    spread = exponent_of(summed)
    total = lax.dynamic_index_in_dim(summed, z, axis=0, keepdims=False)
    for shift in sorted(range(1, outer), key=lambda d: (min(d, outer - d), -d)):
        target = lax.dynamic_index_in_dim(summed, (z + shift) % outer, axis=0, keepdims=False)
        perm = [(2 * q + p, 2 * ((q + shift) % outer) + p) for q in range(outer) for p in range(2)]
        total = total + send(target, perm, spread)
    return with_layout_constraint(total, Layout((0, 1))).T


def gather_over_seq(block, cot, width):
    count = lax.axis_size("seq")
    me = lax.axis_index("seq")
    bits = count.bit_length() - 1
    rows = cot.shape[0]
    last = cot[rows - width :]
    first = cot[:width]
    odd = me % 2 == 1
    stack = block[None]
    for bit in reversed(range(1, bits)):
        pairs = [(i, i ^ (1 << bit)) for i in range(count)]
        stack = jnp.concatenate([stack, lax.ppermute(stack, "seq", pairs)], axis=0)
    piece = jnp.where(odd, first, last)
    outgoing = jnp.concatenate([stack.reshape(-1, block.shape[-1]), piece], axis=0)
    incoming = lax.ppermute(outgoing, "seq", [(i, i ^ 1) for i in range(count)])
    near = incoming[-width:]
    stack = jnp.concatenate([stack, incoming[:-width].reshape(stack.shape)], axis=0)
    across = [(i, i + 1) for i in range(1, count - 1, 2)] + [(i, i - 1) for i in range(2, count, 2)]
    far = lax.ppermute(jnp.where(odd, last, first), "seq", across)
    before = jnp.where(odd, near, far)
    after = jnp.where(odd, far, near)
    extended = jnp.concatenate([before, cot, after], axis=0)
    reverse = jnp.array([int(format(v, "0%db" % bits)[::-1], 2) for v in range(count)], jnp.int32)
    order = reverse[jnp.bitwise_xor(me, jnp.arange(count, dtype=jnp.int32))]
    return jnp.take(stack, order, axis=0).reshape(-1, block.shape[-1]), extended


def body(inputs, cotangent, weight):
    middle_offset = KW // 2
    reach = middle_offset * TAP_SPACING
    length = inputs.shape[1]
    in_width = inputs.shape[2]
    values = inputs[0].astype(jnp.float32)
    activation, deriv = gelu_factors(values)
    act = activation.astype(jnp.bfloat16)
    seq_count = lax.axis_size("seq")
    batch_count = lax.axis_size("batch")
    counted = batch_count * inputs.shape[0] * length * seq_count
    factor = 1.0 / math.sqrt(float(counted))
    channels = cotangent[0].T.reshape(seq_count, -1, length)
    arrived = lax.all_to_all(channels, "seq", 0, 0, tiled=True)
    own_rows = arrived.shape[1]
    owned = jnp.transpose(arrived, (1, 0, 2)).reshape(own_rows, -1)
    if seq_count >= 2 and seq_count & (seq_count - 1) == 0:
        whole_act, extended = gather_over_seq(act, cotangent[0], reach)
    else:
        whole_act = lax.all_gather(act[None], "seq", axis=1, tiled=True)[0]
        extended = extended_2(cotangent, (("seq", 1),), reach)[0]
    count = whole_act.shape[0]
    act_padded = jnp.pad(whole_act, ((reach, reach), (0, 0)))
    updated = []
    for tap_index in range(KW):
        window = lax.slice_in_dim(act_padded, tap_index * TAP_SPACING, tap_index * TAP_SPACING + count, axis=0)
        updated.append(
            lax.dot_general(
                window, owned, (((0,), (1,)), ((), ())), preferred_element_type=jnp.float32
            )
        )
    local_columns = jnp.concatenate(updated, axis=0) * factor
    local_columns = with_layout_constraint(local_columns, Layout((0, 1)))
    local_columns, extended, deriv = lax.optimization_barrier((local_columns, extended, deriv))
    grad_act = jnp.zeros((length, in_width), jnp.float32)
    for tap_index in range(KW):
        window_start = (2 * middle_offset - tap_index) * TAP_SPACING
        window = lax.slice_in_dim(extended, window_start, window_start + length, axis=0)
        grad_act = grad_act + jnp.dot(
            window,
            weight[:, tap_index * in_width : (tap_index + 1) * in_width],
            preferred_element_type=jnp.float32,
        )
    grad_input = (grad_act * deriv).astype(jnp.bfloat16)[None]
    if batch_count == 8:
        grad_weight = reduce_over_batch(local_columns)
    else:
        pieces = local_columns.reshape(batch_count, -1, own_rows)
        swapped = lax.all_to_all(pieces, "batch", split_axis=0, concat_axis=0, tiled=True)
        grad_weight = jnp.sum(swapped, axis=0).T
    return (grad_input, grad_weight)


def solution(mesh):
    placed = (P("batch", "seq", None), P("batch", "seq", None), P())
    return jax.shard_map(
        body,
        mesh=mesh,
        in_specs=placed,
        out_specs=(P("batch", "seq", None), P("seq", "batch")),
        check_vma=False,
    )
```

```python
import math

import jax
import jax.numpy as jnp
from jax import lax
from jax.experimental.layout import Layout, with_layout_constraint
from jax.sharding import PartitionSpec as P

KW = 3
TAP_SPACING = 64
HEADROOM = 12.0
TAG = 16


def extended_2(x, sides, width):
    for axis, dim in sides:
        peers, length = (lax.axis_size(axis), x.shape[dim])
        up = [(i, (i + 1) % peers) for i in range(peers - 1)]
        down = [(j, i) for i, j in up]
        last = lax.slice_in_dim(x, length - width, length, axis=dim)
        first = lax.slice_in_dim(x, 0, width, axis=dim)
        before = lax.ppermute(last, axis, up)
        after = lax.ppermute(first, axis, down)
        x = jnp.concatenate([before, x, after], axis=dim)
    return x


def gelu_factors(values):
    normal_cdf = 0.5 * (1.0 + jax.scipy.special.erf(values / math.sqrt(2.0)))
    density = jnp.exp(-0.5 * values * values) / math.sqrt(2.0 * math.pi)
    return (values * normal_cdf, normal_cdf + values * density)


def exponent_of(values):
    flat = values.reshape(-1, values.shape[-1])
    biggest = jnp.max(jnp.max(jnp.abs(flat), axis=0, keepdims=True), axis=1, keepdims=True)
    return jnp.floor(jnp.log2(jnp.maximum(biggest, 1e-30)))


def encode(values, exponent):
    flat = values.reshape(-1, values.shape[-1])
    scaled = (flat * jnp.exp2(HEADROOM - exponent)).astype(jnp.float16)
    tag = jnp.broadcast_to(exponent.astype(jnp.float16), (TAG, flat.shape[-1]))
    return with_layout_constraint(jnp.concatenate([scaled, tag], axis=0), Layout((0, 1)))


def decode(packed, shape):
    exponent = packed[-TAG:1 - TAG, 0:1].astype(jnp.float32)
    values = packed[:-TAG].astype(jnp.float32) * jnp.exp2(exponent - HEADROOM)
    return values.reshape(shape)


def send(values, perm, exponent):
    arrived = lax.ppermute(encode(values, exponent), "batch", perm)
    return decode(with_layout_constraint(arrived, Layout((0, 1))), values.shape)


def reduce_over_batch(columns):
    count = lax.axis_size("batch")
    outer = count // 2
    me = lax.axis_index("batch")
    x = me % 2
    z = me // 2
    blocks = columns.reshape(outer, 2, -1, columns.shape[1])
    exponent = exponent_of(columns)
    acc = lax.dynamic_index_in_dim(blocks, z, axis=0, keepdims=False)
    for shift in sorted(range(1, outer), key=lambda d: (min(d, outer - d), -d)):
        target = lax.dynamic_index_in_dim(blocks, (z + shift) % outer, axis=0, keepdims=False)
        perm = [(2 * q + p, 2 * ((q + shift) % outer) + p) for q in range(outer) for p in range(2)]
        acc = acc + send(target, perm, exponent)
    acc = with_layout_constraint(acc, Layout((0, 1, 2)))
    mine = lax.dynamic_index_in_dim(acc, x, axis=0, keepdims=False)
    theirs = lax.dynamic_index_in_dim(acc, 1 - x, axis=0, keepdims=False)
    total = mine + send(theirs, [(i, i ^ 1) for i in range(count)], exponent_of(theirs))
    return with_layout_constraint(total, Layout((0, 1))).T


def gather_over_seq(block, cot, width):
    count = lax.axis_size("seq")
    me = lax.axis_index("seq")
    bits = count.bit_length() - 1
    rows = cot.shape[0]
    last = cot[rows - width :]
    first = cot[:width]
    odd = me % 2 == 1
    stack = block[None]
    for bit in reversed(range(1, bits)):
        pairs = [(i, i ^ (1 << bit)) for i in range(count)]
        stack = jnp.concatenate([stack, lax.ppermute(stack, "seq", pairs)], axis=0)
    piece = jnp.where(odd, first, last)
    outgoing = jnp.concatenate([stack.reshape(-1, block.shape[-1]), piece], axis=0)
    incoming = lax.ppermute(outgoing, "seq", [(i, i ^ 1) for i in range(count)])
    near = incoming[-width:]
    stack = jnp.concatenate([stack, incoming[:-width].reshape(stack.shape)], axis=0)
    across = [(i, i + 1) for i in range(1, count - 1, 2)] + [(i, i - 1) for i in range(2, count, 2)]
    far = lax.ppermute(jnp.where(odd, last, first), "seq", across)
    before = jnp.where(odd, near, far)
    after = jnp.where(odd, far, near)
    extended = jnp.concatenate([before, cot, after], axis=0)
    reverse = jnp.array([int(format(v, "0%db" % bits)[::-1], 2) for v in range(count)], jnp.int32)
    order = reverse[jnp.bitwise_xor(me, jnp.arange(count, dtype=jnp.int32))]
    return jnp.take(stack, order, axis=0).reshape(-1, block.shape[-1]), extended


def body(inputs, cotangent, weight):
    middle_offset = KW // 2
    reach = middle_offset * TAP_SPACING
    length = inputs.shape[1]
    in_width = inputs.shape[2]
    values = inputs[0].astype(jnp.float32)
    activation, deriv = gelu_factors(values)
    act = activation.astype(jnp.bfloat16)
    seq_count = lax.axis_size("seq")
    batch_count = lax.axis_size("batch")
    counted = batch_count * inputs.shape[0] * length * seq_count
    factor = 1.0 / math.sqrt(float(counted))
    channels = cotangent[0].T.reshape(seq_count, -1, length)
    arrived = lax.all_to_all(channels, "seq", 0, 0, tiled=True)
    own_rows = arrived.shape[1]
    owned = jnp.transpose(arrived, (1, 0, 2)).reshape(own_rows, -1)
    if seq_count >= 2 and seq_count & (seq_count - 1) == 0:
        whole_act, extended = gather_over_seq(act, cotangent[0], reach)
    else:
        whole_act = lax.all_gather(act[None], "seq", axis=1, tiled=True)[0]
        extended = extended_2(cotangent, (("seq", 1),), reach)[0]
    count = whole_act.shape[0]
    act_padded = jnp.pad(whole_act, ((reach, reach), (0, 0)))
    updated = []
    for tap_index in range(KW):
        window = lax.slice_in_dim(act_padded, tap_index * TAP_SPACING, tap_index * TAP_SPACING + count, axis=0)
        updated.append(
            lax.dot_general(
                window, owned, (((0,), (1,)), ((), ())), preferred_element_type=jnp.float32
            )
        )
    local_columns = jnp.concatenate(updated, axis=0) * factor
    local_columns = with_layout_constraint(local_columns, Layout((0, 1)))
    local_columns, extended, deriv = lax.optimization_barrier((local_columns, extended, deriv))
    grad_act = jnp.zeros((length, in_width), jnp.float32)
    for tap_index in range(KW):
        window_start = (2 * middle_offset - tap_index) * TAP_SPACING
        window = lax.slice_in_dim(extended, window_start, window_start + length, axis=0)
        grad_act = grad_act + jnp.dot(
            window,
            weight[:, tap_index * in_width : (tap_index + 1) * in_width],
            preferred_element_type=jnp.float32,
        )
    grad_input = (grad_act * deriv).astype(jnp.bfloat16)[None]
    if batch_count == 8:
        grad_weight = reduce_over_batch(local_columns)
    else:
        pieces = local_columns.reshape(batch_count, -1, own_rows)
        swapped = lax.all_to_all(pieces, "batch", split_axis=0, concat_axis=0, tiled=True)
        grad_weight = jnp.sum(swapped, axis=0).T
    return (grad_input, grad_weight)


def solution(mesh):
    placed = (P("batch", "seq", None), P("batch", "seq", None), P())
    return jax.shard_map(
        body,
        mesh=mesh,
        in_specs=placed,
        out_specs=(P("batch", "seq", None), P("seq", "batch")),
        check_vma=False,
    )
```

```python
import math

import jax
import jax.numpy as jnp
from jax import lax
from jax.experimental.layout import Layout, with_layout_constraint
from jax.sharding import PartitionSpec as P

KW = 3
TAP_SPACING = 64
HEADROOM = 12.0
TAG = 16


def extended_2(x, sides, width):
    for axis, dim in sides:
        peers, length = (lax.axis_size(axis), x.shape[dim])
        up = [(i, (i + 1) % peers) for i in range(peers - 1)]
        down = [(j, i) for i, j in up]
        last = lax.slice_in_dim(x, length - width, length, axis=dim)
        first = lax.slice_in_dim(x, 0, width, axis=dim)
        before = lax.ppermute(last, axis, up)
        after = lax.ppermute(first, axis, down)
        x = jnp.concatenate([before, x, after], axis=dim)
    return x


def gelu_factors(values):
    normal_cdf = 0.5 * (1.0 + jax.scipy.special.erf(values / math.sqrt(2.0)))
    density = jnp.exp(-0.5 * values * values) / math.sqrt(2.0 * math.pi)
    return (values * normal_cdf, normal_cdf + values * density)


def exponent_of(values):
    flat = values.reshape(-1, values.shape[-1])
    biggest = jnp.max(jnp.max(jnp.abs(flat), axis=0, keepdims=True), axis=1, keepdims=True)
    return jnp.floor(jnp.log2(jnp.maximum(biggest, 1e-30)))


def encode(values, exponent):
    flat = values.reshape(-1, values.shape[-1])
    scaled = (flat * jnp.exp2(HEADROOM - exponent)).astype(jnp.float16)
    tag = jnp.broadcast_to(exponent.astype(jnp.float16), (TAG, flat.shape[-1]))
    return with_layout_constraint(jnp.concatenate([scaled, tag], axis=0), Layout((0, 1)))


def decode(packed, shape):
    exponent = packed[-TAG:1 - TAG].astype(jnp.float32)
    values = packed[:-TAG].astype(jnp.float32) * jnp.exp2(exponent - HEADROOM)
    return values.reshape(shape)


def send(values, perm, exponent):
    arrived = lax.ppermute(encode(values, exponent), "batch", perm)
    return decode(with_layout_constraint(arrived, Layout((0, 1))), values.shape)


def reduce_over_batch(columns):
    count = lax.axis_size("batch")
    outer = count // 2
    me = lax.axis_index("batch")
    x = me % 2
    z = me // 2
    pairs = [(i, i ^ 1) for i in range(count)]
    blocks = columns.reshape(outer, 2, -1, columns.shape[1])
    mine = lax.dynamic_index_in_dim(blocks, x, axis=1, keepdims=False)
    theirs = lax.dynamic_index_in_dim(blocks, 1 - x, axis=1, keepdims=False)
    summed = with_layout_constraint(mine + send(theirs, pairs, exponent_of(theirs)), Layout((0, 1, 2)))
    spread = exponent_of(summed)
    total = lax.dynamic_index_in_dim(summed, z, axis=0, keepdims=False)
    for shift in sorted(range(1, outer), key=lambda d: (min(d, outer - d), -d)):
        target = lax.dynamic_index_in_dim(summed, (z + shift) % outer, axis=0, keepdims=False)
        perm = [(2 * q + p, 2 * ((q + shift) % outer) + p) for q in range(outer) for p in range(2)]
        total = total + send(target, perm, spread)
    return with_layout_constraint(total, Layout((0, 1))).T


def gather_over_seq(block, cot, width):
    count = lax.axis_size("seq")
    me = lax.axis_index("seq")
    bits = count.bit_length() - 1
    rows = cot.shape[0]
    last = cot[rows - width :]
    first = cot[:width]
    odd = me % 2 == 1
    stack = block[None]
    for bit in reversed(range(1, bits)):
        pairs = [(i, i ^ (1 << bit)) for i in range(count)]
        stack = jnp.concatenate([stack, lax.ppermute(stack, "seq", pairs)], axis=0)
    piece = jnp.where(odd, first, last)
    outgoing = jnp.concatenate([stack.reshape(-1, block.shape[-1]), piece], axis=0)
    incoming = lax.ppermute(outgoing, "seq", [(i, i ^ 1) for i in range(count)])
    near = incoming[-width:]
    stack = jnp.concatenate([stack, incoming[:-width].reshape(stack.shape)], axis=0)
    across = [(i, i + 1) for i in range(1, count - 1, 2)] + [(i, i - 1) for i in range(2, count, 2)]
    far = lax.ppermute(jnp.where(odd, last, first), "seq", across)
    before = jnp.where(odd, near, far)
    after = jnp.where(odd, far, near)
    extended = jnp.concatenate([before, cot, after], axis=0)
    reverse = jnp.array([int(format(v, "0%db" % bits)[::-1], 2) for v in range(count)], jnp.int32)
    order = reverse[jnp.bitwise_xor(me, jnp.arange(count, dtype=jnp.int32))]
    return jnp.take(stack, order, axis=0).reshape(-1, block.shape[-1]), extended


def body(inputs, cotangent, weight):
    middle_offset = KW // 2
    reach = middle_offset * TAP_SPACING
    length = inputs.shape[1]
    in_width = inputs.shape[2]
    values = inputs[0].astype(jnp.float32)
    activation, deriv = gelu_factors(values)
    act = activation.astype(jnp.bfloat16)
    seq_count = lax.axis_size("seq")
    batch_count = lax.axis_size("batch")
    counted = batch_count * inputs.shape[0] * length * seq_count
    factor = 1.0 / math.sqrt(float(counted))
    channels = cotangent[0].T.reshape(seq_count, -1, length)
    arrived = lax.all_to_all(channels, "seq", 0, 0, tiled=True)
    own_rows = arrived.shape[1]
    owned = jnp.transpose(arrived, (1, 0, 2)).reshape(own_rows, -1)
    if seq_count >= 2 and seq_count & (seq_count - 1) == 0:
        whole_act, extended = gather_over_seq(act, cotangent[0], reach)
    else:
        whole_act = lax.all_gather(act[None], "seq", axis=1, tiled=True)[0]
        extended = extended_2(cotangent, (("seq", 1),), reach)[0]
    count = whole_act.shape[0]
    act_padded = jnp.pad(whole_act, ((reach, reach), (0, 0)))
    updated = []
    for tap_index in range(KW):
        window = lax.slice_in_dim(act_padded, tap_index * TAP_SPACING, tap_index * TAP_SPACING + count, axis=0)
        updated.append(
            lax.dot_general(
                window, owned, (((0,), (1,)), ((), ())), preferred_element_type=jnp.float32
            )
        )
    local_columns = jnp.concatenate(updated, axis=0) * factor
    local_columns = with_layout_constraint(local_columns, Layout((0, 1)))
    local_columns, extended, deriv = lax.optimization_barrier((local_columns, extended, deriv))
    grad_act = jnp.zeros((length, in_width), jnp.float32)
    for tap_index in range(KW):
        window_start = (2 * middle_offset - tap_index) * TAP_SPACING
        window = lax.slice_in_dim(extended, window_start, window_start + length, axis=0)
        grad_act = grad_act + jnp.dot(
            window,
            weight[:, tap_index * in_width : (tap_index + 1) * in_width],
            preferred_element_type=jnp.float32,
        )
    grad_input = (grad_act * deriv).astype(jnp.bfloat16)[None]
    if batch_count == 8:
        grad_weight = reduce_over_batch(local_columns)
    else:
        pieces = local_columns.reshape(batch_count, -1, own_rows)
        swapped = lax.all_to_all(pieces, "batch", split_axis=0, concat_axis=0, tiled=True)
        grad_weight = jnp.sum(swapped, axis=0).T
    return (grad_input, grad_weight)


def solution(mesh):
    placed = (P("batch", "seq", None), P("batch", "seq", None), P())
    return jax.shard_map(
        body,
        mesh=mesh,
        in_specs=placed,
        out_specs=(P("batch", "seq", None), P("seq", "batch")),
        check_vma=False,
    )
```

```python
import math

import jax
import jax.numpy as jnp
from jax import lax
from jax.experimental.layout import Layout, with_layout_constraint
from jax.sharding import PartitionSpec as P

KW = 3
TAP_SPACING = 64
HEADROOM = 12.0
TAG = 16


def extended_2(x, sides, width):
    for axis, dim in sides:
        peers, length = (lax.axis_size(axis), x.shape[dim])
        up = [(i, (i + 1) % peers) for i in range(peers - 1)]
        down = [(j, i) for i, j in up]
        last = lax.slice_in_dim(x, length - width, length, axis=dim)
        first = lax.slice_in_dim(x, 0, width, axis=dim)
        before = lax.ppermute(last, axis, up)
        after = lax.ppermute(first, axis, down)
        x = jnp.concatenate([before, x, after], axis=dim)
    return x


def gelu_factors(values):
    normal_cdf = 0.5 * (1.0 + jax.scipy.special.erf(values / math.sqrt(2.0)))
    density = jnp.exp(-0.5 * values * values) / math.sqrt(2.0 * math.pi)
    return (values * normal_cdf, normal_cdf + values * density)


def exponent_of(values):
    flat = values.reshape(-1, values.shape[-1])
    biggest = jnp.max(jnp.abs(flat), axis=0, keepdims=True)
    return jnp.floor(jnp.log2(jnp.maximum(biggest, 1e-30)))


def encode(values, exponent):
    flat = values.reshape(-1, values.shape[-1])
    scaled = (flat * jnp.exp2(HEADROOM - exponent)).astype(jnp.float16)
    tag = jnp.broadcast_to(exponent.astype(jnp.float16), (TAG, flat.shape[-1]))
    return with_layout_constraint(jnp.concatenate([scaled, tag], axis=0), Layout((0, 1)))


def decode(packed, shape):
    exponent = packed[-TAG:1 - TAG].astype(jnp.float32)
    values = packed[:-TAG].astype(jnp.float32) * jnp.exp2(exponent - HEADROOM)
    return values.reshape(shape)


def send(values, perm, exponent):
    arrived = lax.ppermute(encode(values, exponent), "batch", perm)
    return decode(with_layout_constraint(arrived, Layout((0, 1))), values.shape)


def reduce_over_batch(columns):
    count = lax.axis_size("batch")
    outer = count // 2
    me = lax.axis_index("batch")
    x = me % 2
    z = me // 2
    pairs = [(i, i ^ 1) for i in range(count)]
    blocks = columns.reshape(outer, 2, -1, columns.shape[1])
    mine = lax.dynamic_index_in_dim(blocks, x, axis=1, keepdims=False)
    theirs = lax.dynamic_index_in_dim(blocks, 1 - x, axis=1, keepdims=False)
    summed = with_layout_constraint(mine + send(theirs, pairs, exponent_of(theirs)), Layout((0, 1, 2)))
    spread = exponent_of(summed)
    total = lax.dynamic_index_in_dim(summed, z, axis=0, keepdims=False)
    for shift in sorted(range(1, outer), key=lambda d: (min(d, outer - d), -d)):
        target = lax.dynamic_index_in_dim(summed, (z + shift) % outer, axis=0, keepdims=False)
        perm = [(2 * q + p, 2 * ((q + shift) % outer) + p) for q in range(outer) for p in range(2)]
        total = total + send(target, perm, spread)
    return with_layout_constraint(total, Layout((0, 1))).T


def gather_over_seq(block, cot, width):
    count = lax.axis_size("seq")
    me = lax.axis_index("seq")
    bits = count.bit_length() - 1
    rows = cot.shape[0]
    last = cot[rows - width :]
    first = cot[:width]
    odd = me % 2 == 1
    stack = block[None]
    for bit in reversed(range(1, bits)):
        pairs = [(i, i ^ (1 << bit)) for i in range(count)]
        stack = jnp.concatenate([stack, lax.ppermute(stack, "seq", pairs)], axis=0)
    piece = jnp.where(odd, first, last)
    outgoing = jnp.concatenate([stack.reshape(-1, block.shape[-1]), piece], axis=0)
    incoming = lax.ppermute(outgoing, "seq", [(i, i ^ 1) for i in range(count)])
    near = incoming[-width:]
    stack = jnp.concatenate([stack, incoming[:-width].reshape(stack.shape)], axis=0)
    across = [(i, i + 1) for i in range(1, count - 1, 2)] + [(i, i - 1) for i in range(2, count, 2)]
    far = lax.ppermute(jnp.where(odd, last, first), "seq", across)
    before = jnp.where(odd, near, far)
    after = jnp.where(odd, far, near)
    extended = jnp.concatenate([before, cot, after], axis=0)
    reverse = jnp.array([int(format(v, "0%db" % bits)[::-1], 2) for v in range(count)], jnp.int32)
    order = reverse[jnp.bitwise_xor(me, jnp.arange(count, dtype=jnp.int32))]
    return jnp.take(stack, order, axis=0).reshape(-1, block.shape[-1]), extended


def body(inputs, cotangent, weight):
    middle_offset = KW // 2
    reach = middle_offset * TAP_SPACING
    length = inputs.shape[1]
    in_width = inputs.shape[2]
    values = inputs[0].astype(jnp.float32)
    activation, deriv = gelu_factors(values)
    act = activation.astype(jnp.bfloat16)
    seq_count = lax.axis_size("seq")
    batch_count = lax.axis_size("batch")
    counted = batch_count * inputs.shape[0] * length * seq_count
    factor = 1.0 / math.sqrt(float(counted))
    channels = cotangent[0].T.reshape(seq_count, -1, length)
    arrived = lax.all_to_all(channels, "seq", 0, 0, tiled=True)
    own_rows = arrived.shape[1]
    owned = jnp.transpose(arrived, (1, 0, 2)).reshape(own_rows, -1)
    if seq_count >= 2 and seq_count & (seq_count - 1) == 0:
        whole_act, extended = gather_over_seq(act, cotangent[0], reach)
    else:
        whole_act = lax.all_gather(act[None], "seq", axis=1, tiled=True)[0]
        extended = extended_2(cotangent, (("seq", 1),), reach)[0]
    count = whole_act.shape[0]
    act_padded = jnp.pad(whole_act, ((reach, reach), (0, 0)))
    updated = []
    for tap_index in range(KW):
        window = lax.slice_in_dim(act_padded, tap_index * TAP_SPACING, tap_index * TAP_SPACING + count, axis=0)
        updated.append(
            lax.dot_general(
                window, owned, (((0,), (1,)), ((), ())), preferred_element_type=jnp.float32
            )
        )
    local_columns = jnp.concatenate(updated, axis=0) * factor
    local_columns = with_layout_constraint(local_columns, Layout((0, 1)))
    local_columns, extended, deriv = lax.optimization_barrier((local_columns, extended, deriv))
    grad_act = jnp.zeros((length, in_width), jnp.float32)
    for tap_index in range(KW):
        window_start = (2 * middle_offset - tap_index) * TAP_SPACING
        window = lax.slice_in_dim(extended, window_start, window_start + length, axis=0)
        grad_act = grad_act + jnp.dot(
            window,
            weight[:, tap_index * in_width : (tap_index + 1) * in_width],
            preferred_element_type=jnp.float32,
        )
    grad_input = (grad_act * deriv).astype(jnp.bfloat16)[None]
    if batch_count == 8:
        grad_weight = reduce_over_batch(local_columns)
    else:
        pieces = local_columns.reshape(batch_count, -1, own_rows)
        swapped = lax.all_to_all(pieces, "batch", split_axis=0, concat_axis=0, tiled=True)
        grad_weight = jnp.sum(swapped, axis=0).T
    return (grad_input, grad_weight)


def solution(mesh):
    placed = (P("batch", "seq", None), P("batch", "seq", None), P())
    return jax.shard_map(
        body,
        mesh=mesh,
        in_specs=placed,
        out_specs=(P("batch", "seq", None), P("seq", "batch")),
        check_vma=False,
    )
```

```python
import math

import jax
import jax.numpy as jnp
from jax import lax
from jax.experimental.layout import Layout, with_layout_constraint
from jax.sharding import PartitionSpec as P

KW = 3
TAP_SPACING = 64
HEADROOM = 12.0
TAG = 16


def extended_2(x, sides, width):
    for axis, dim in sides:
        peers, length = (lax.axis_size(axis), x.shape[dim])
        up = [(i, (i + 1) % peers) for i in range(peers - 1)]
        down = [(j, i) for i, j in up]
        last = lax.slice_in_dim(x, length - width, length, axis=dim)
        first = lax.slice_in_dim(x, 0, width, axis=dim)
        before = lax.ppermute(last, axis, up)
        after = lax.ppermute(first, axis, down)
        x = jnp.concatenate([before, x, after], axis=dim)
    return x


def gelu_factors(values):
    normal_cdf = 0.5 * (1.0 + jax.scipy.special.erf(values / math.sqrt(2.0)))
    density = jnp.exp(-0.5 * values * values) / math.sqrt(2.0 * math.pi)
    return (values * normal_cdf, normal_cdf + values * density)


def exponent_of(values):
    flat = values.reshape(-1, values.shape[-1])
    biggest = jnp.max(jnp.abs(flat), axis=0, keepdims=True)
    return jnp.floor(jnp.log2(jnp.maximum(biggest, 1e-30)))


def encode(values, exponent):
    flat = values.reshape(-1, values.shape[-1])
    scaled = (flat * jnp.exp2(HEADROOM - exponent)).astype(jnp.float16)
    tag = jnp.broadcast_to(exponent.astype(jnp.float16), (TAG, flat.shape[-1]))
    return with_layout_constraint(jnp.concatenate([scaled, tag], axis=0), Layout((0, 1)))


def decode(packed, shape):
    exponent = packed[-TAG:1 - TAG].astype(jnp.float32)
    values = packed[:-TAG].astype(jnp.float32) * jnp.exp2(exponent - HEADROOM)
    return values.reshape(shape)


def send(values, perm, exponent):
    arrived = lax.ppermute(encode(values, exponent), "batch", perm)
    return decode(with_layout_constraint(arrived, Layout((0, 1))), values.shape)


def reduce_over_batch(columns):
    count = lax.axis_size("batch")
    outer = count // 2
    me = lax.axis_index("batch")
    x = me % 2
    z = me // 2
    pairs = [(i, i ^ 1) for i in range(count)]
    blocks = columns.reshape(outer, 2, -1, columns.shape[1])
    mine = lax.dynamic_index_in_dim(blocks, x, axis=1, keepdims=False)
    theirs = lax.dynamic_index_in_dim(blocks, 1 - x, axis=1, keepdims=False)
    half = outer // 2
    received = jnp.concatenate(
        [send(theirs[:half], pairs, exponent_of(theirs[:half])),
         send(theirs[half:], pairs, exponent_of(theirs[half:]))], axis=0
    )
    summed = with_layout_constraint(mine + received, Layout((0, 1, 2)))
    spread = exponent_of(summed)
    total = lax.dynamic_index_in_dim(summed, z, axis=0, keepdims=False)
    for shift in sorted(range(1, outer), key=lambda d: (min(d, outer - d), -d)):
        target = lax.dynamic_index_in_dim(summed, (z + shift) % outer, axis=0, keepdims=False)
        perm = [(2 * q + p, 2 * ((q + shift) % outer) + p) for q in range(outer) for p in range(2)]
        total = total + send(target, perm, spread)
    return with_layout_constraint(total, Layout((0, 1))).T


def gather_over_seq(block, cot, width):
    count = lax.axis_size("seq")
    me = lax.axis_index("seq")
    bits = count.bit_length() - 1
    rows = cot.shape[0]
    last = cot[rows - width :]
    first = cot[:width]
    odd = me % 2 == 1
    stack = block[None]
    for bit in reversed(range(1, bits)):
        pairs = [(i, i ^ (1 << bit)) for i in range(count)]
        stack = jnp.concatenate([stack, lax.ppermute(stack, "seq", pairs)], axis=0)
    piece = jnp.where(odd, first, last)
    outgoing = jnp.concatenate([stack.reshape(-1, block.shape[-1]), piece], axis=0)
    incoming = lax.ppermute(outgoing, "seq", [(i, i ^ 1) for i in range(count)])
    near = incoming[-width:]
    stack = jnp.concatenate([stack, incoming[:-width].reshape(stack.shape)], axis=0)
    across = [(i, i + 1) for i in range(1, count - 1, 2)] + [(i, i - 1) for i in range(2, count, 2)]
    far = lax.ppermute(jnp.where(odd, last, first), "seq", across)
    before = jnp.where(odd, near, far)
    after = jnp.where(odd, far, near)
    extended = jnp.concatenate([before, cot, after], axis=0)
    reverse = jnp.array([int(format(v, "0%db" % bits)[::-1], 2) for v in range(count)], jnp.int32)
    order = reverse[jnp.bitwise_xor(me, jnp.arange(count, dtype=jnp.int32))]
    return jnp.take(stack, order, axis=0).reshape(-1, block.shape[-1]), extended


def body(inputs, cotangent, weight):
    middle_offset = KW // 2
    reach = middle_offset * TAP_SPACING
    length = inputs.shape[1]
    in_width = inputs.shape[2]
    values = inputs[0].astype(jnp.float32)
    activation, deriv = gelu_factors(values)
    act = activation.astype(jnp.bfloat16)
    seq_count = lax.axis_size("seq")
    batch_count = lax.axis_size("batch")
    counted = batch_count * inputs.shape[0] * length * seq_count
    factor = 1.0 / math.sqrt(float(counted))
    channels = cotangent[0].T.reshape(seq_count, -1, length)
    arrived = lax.all_to_all(channels, "seq", 0, 0, tiled=True)
    own_rows = arrived.shape[1]
    owned = jnp.transpose(arrived, (1, 0, 2)).reshape(own_rows, -1)
    if seq_count >= 2 and seq_count & (seq_count - 1) == 0:
        whole_act, extended = gather_over_seq(act, cotangent[0], reach)
    else:
        whole_act = lax.all_gather(act[None], "seq", axis=1, tiled=True)[0]
        extended = extended_2(cotangent, (("seq", 1),), reach)[0]
    count = whole_act.shape[0]
    act_padded = jnp.pad(whole_act, ((reach, reach), (0, 0)))
    updated = []
    for tap_index in range(KW):
        window = lax.slice_in_dim(act_padded, tap_index * TAP_SPACING, tap_index * TAP_SPACING + count, axis=0)
        updated.append(
            lax.dot_general(
                window, owned, (((0,), (1,)), ((), ())), preferred_element_type=jnp.float32
            )
        )
    local_columns = jnp.concatenate(updated, axis=0) * factor
    local_columns = with_layout_constraint(local_columns, Layout((0, 1)))
    local_columns, extended, deriv = lax.optimization_barrier((local_columns, extended, deriv))
    grad_act = jnp.zeros((length, in_width), jnp.float32)
    for tap_index in range(KW):
        window_start = (2 * middle_offset - tap_index) * TAP_SPACING
        window = lax.slice_in_dim(extended, window_start, window_start + length, axis=0)
        grad_act = grad_act + jnp.dot(
            window,
            weight[:, tap_index * in_width : (tap_index + 1) * in_width],
            preferred_element_type=jnp.float32,
        )
    grad_input = (grad_act * deriv).astype(jnp.bfloat16)[None]
    if batch_count == 8:
        grad_weight = reduce_over_batch(local_columns)
    else:
        pieces = local_columns.reshape(batch_count, -1, own_rows)
        swapped = lax.all_to_all(pieces, "batch", split_axis=0, concat_axis=0, tiled=True)
        grad_weight = jnp.sum(swapped, axis=0).T
    return (grad_input, grad_weight)


def solution(mesh):
    placed = (P("batch", "seq", None), P("batch", "seq", None), P())
    return jax.shard_map(
        body,
        mesh=mesh,
        in_specs=placed,
        out_specs=(P("batch", "seq", None), P("seq", "batch")),
        check_vma=False,
    )
```

```python
import math

import jax
import jax.numpy as jnp
from jax import lax
from jax.experimental.layout import Layout, with_layout_constraint
from jax.sharding import PartitionSpec as P

KW = 3
TAP_SPACING = 64
HEADROOM = 12.0
TAG = 16


def extended_2(x, sides, width):
    for axis, dim in sides:
        peers, length = (lax.axis_size(axis), x.shape[dim])
        up = [(i, (i + 1) % peers) for i in range(peers - 1)]
        down = [(j, i) for i, j in up]
        last = lax.slice_in_dim(x, length - width, length, axis=dim)
        first = lax.slice_in_dim(x, 0, width, axis=dim)
        before = lax.ppermute(last, axis, up)
        after = lax.ppermute(first, axis, down)
        x = jnp.concatenate([before, x, after], axis=dim)
    return x


def gelu_factors(values):
    normal_cdf = 0.5 * (1.0 + jax.scipy.special.erf(values / math.sqrt(2.0)))
    density = jnp.exp(-0.5 * values * values) / math.sqrt(2.0 * math.pi)
    return (values * normal_cdf, normal_cdf + values * density)


def exponent_of(values):
    flat = values.reshape(-1, values.shape[-1])
    biggest = jnp.max(jnp.abs(flat), axis=0, keepdims=True)
    return jnp.floor(jnp.log2(jnp.maximum(biggest, 1e-30)))


def encode(values, exponent):
    flat = values.reshape(-1, values.shape[-1])
    scaled = (flat * jnp.exp2(HEADROOM - exponent)).astype(jnp.float16)
    tag = jnp.broadcast_to(exponent.astype(jnp.float16), (TAG, flat.shape[-1]))
    return with_layout_constraint(jnp.concatenate([scaled, tag], axis=0), Layout((0, 1)))


def decode(packed, shape):
    exponent = packed[-TAG:1 - TAG].astype(jnp.float32)
    values = packed[:-TAG].astype(jnp.float32) * jnp.exp2(exponent - HEADROOM)
    return values.reshape(shape)


def send(values, perm, exponent):
    arrived = lax.ppermute(encode(values, exponent), "batch", perm)
    return decode(with_layout_constraint(arrived, Layout((0, 1))), values.shape)


def reduce_over_batch(columns, rider):
    count = lax.axis_size("batch")
    outer = count // 2
    me = lax.axis_index("batch")
    x = me % 2
    z = me // 2
    pairs = [(i, i ^ 1) for i in range(count)]
    blocks = columns.reshape(outer, 2, -1, columns.shape[1])
    mine = lax.dynamic_index_in_dim(blocks, x, axis=1, keepdims=False)
    theirs = lax.dynamic_index_in_dim(blocks, 1 - x, axis=1, keepdims=False)
    half = outer // 2
    received = jnp.concatenate(
        [send(theirs[:half], pairs, exponent_of(theirs[:half])),
         send(theirs[half:], pairs, exponent_of(theirs[half:]))], axis=0
    )
    received, rider = lax.optimization_barrier((received, rider))
    summed = with_layout_constraint(mine + received, Layout((0, 1, 2)))
    spread = exponent_of(summed)
    total = lax.dynamic_index_in_dim(summed, z, axis=0, keepdims=False)
    for shift in sorted(range(1, outer), key=lambda d: (min(d, outer - d), -d)):
        target = lax.dynamic_index_in_dim(summed, (z + shift) % outer, axis=0, keepdims=False)
        perm = [(2 * q + p, 2 * ((q + shift) % outer) + p) for q in range(outer) for p in range(2)]
        total = total + send(target, perm, spread)
    return with_layout_constraint(total, Layout((0, 1))).T, rider


def gather_over_seq(block, cot, width):
    count = lax.axis_size("seq")
    me = lax.axis_index("seq")
    bits = count.bit_length() - 1
    rows = cot.shape[0]
    last = cot[rows - width :]
    first = cot[:width]
    odd = me % 2 == 1
    stack = block[None]
    for bit in reversed(range(1, bits)):
        pairs = [(i, i ^ (1 << bit)) for i in range(count)]
        stack = jnp.concatenate([stack, lax.ppermute(stack, "seq", pairs)], axis=0)
    piece = jnp.where(odd, first, last)
    outgoing = jnp.concatenate([stack.reshape(-1, block.shape[-1]), piece], axis=0)
    incoming = lax.ppermute(outgoing, "seq", [(i, i ^ 1) for i in range(count)])
    near = incoming[-width:]
    stack = jnp.concatenate([stack, incoming[:-width].reshape(stack.shape)], axis=0)
    across = [(i, i + 1) for i in range(1, count - 1, 2)] + [(i, i - 1) for i in range(2, count, 2)]
    far = lax.ppermute(jnp.where(odd, last, first), "seq", across)
    before = jnp.where(odd, near, far)
    after = jnp.where(odd, far, near)
    extended = jnp.concatenate([before, cot, after], axis=0)
    reverse = jnp.array([int(format(v, "0%db" % bits)[::-1], 2) for v in range(count)], jnp.int32)
    order = reverse[jnp.bitwise_xor(me, jnp.arange(count, dtype=jnp.int32))]
    return jnp.take(stack, order, axis=0).reshape(-1, block.shape[-1]), extended


def body(inputs, cotangent, weight):
    middle_offset = KW // 2
    reach = middle_offset * TAP_SPACING
    length = inputs.shape[1]
    in_width = inputs.shape[2]
    values = inputs[0].astype(jnp.float32)
    activation, deriv = gelu_factors(values)
    act = activation.astype(jnp.bfloat16)
    seq_count = lax.axis_size("seq")
    batch_count = lax.axis_size("batch")
    counted = batch_count * inputs.shape[0] * length * seq_count
    factor = 1.0 / math.sqrt(float(counted))
    channels = cotangent[0].T.reshape(seq_count, -1, length)
    arrived = lax.all_to_all(channels, "seq", 0, 0, tiled=True)
    own_rows = arrived.shape[1]
    owned = jnp.transpose(arrived, (1, 0, 2)).reshape(own_rows, -1)
    if seq_count >= 2 and seq_count & (seq_count - 1) == 0:
        whole_act, extended = gather_over_seq(act, cotangent[0], reach)
    else:
        whole_act = lax.all_gather(act[None], "seq", axis=1, tiled=True)[0]
        extended = extended_2(cotangent, (("seq", 1),), reach)[0]
    count = whole_act.shape[0]
    act_padded = jnp.pad(whole_act, ((reach, reach), (0, 0)))
    updated = []
    for tap_index in range(KW):
        window = lax.slice_in_dim(act_padded, tap_index * TAP_SPACING, tap_index * TAP_SPACING + count, axis=0)
        updated.append(
            lax.dot_general(
                window, owned, (((0,), (1,)), ((), ())), preferred_element_type=jnp.float32
            )
        )
    local_columns = jnp.concatenate(updated, axis=0) * factor
    local_columns = with_layout_constraint(local_columns, Layout((0, 1)))
    local_columns, extended, deriv = lax.optimization_barrier((local_columns, extended, deriv))
    grad_act = jnp.zeros((length, in_width), jnp.float32)
    for tap_index in range(KW):
        window_start = (2 * middle_offset - tap_index) * TAP_SPACING
        window = lax.slice_in_dim(extended, window_start, window_start + length, axis=0)
        grad_act = grad_act + jnp.dot(
            window,
            weight[:, tap_index * in_width : (tap_index + 1) * in_width],
            preferred_element_type=jnp.float32,
        )
    grad_input = (grad_act * deriv).astype(jnp.bfloat16)[None]
    if batch_count == 8:
        grad_weight, grad_input = reduce_over_batch(local_columns, grad_input)
    else:
        pieces = local_columns.reshape(batch_count, -1, own_rows)
        swapped = lax.all_to_all(pieces, "batch", split_axis=0, concat_axis=0, tiled=True)
        grad_weight = jnp.sum(swapped, axis=0).T
    return (grad_input, grad_weight)


def solution(mesh):
    placed = (P("batch", "seq", None), P("batch", "seq", None), P())
    return jax.shard_map(
        body,
        mesh=mesh,
        in_specs=placed,
        out_specs=(P("batch", "seq", None), P("seq", "batch")),
        check_vma=False,
    )
```
